32 devices in a mesh: row: 8 (over y, x, core), col: 4 (over z).
Axes of the slice: x: 2, y: 2, z: 4, core: 2. Of those that a mesh axis runs over, the one named last changes fastest.
Arguments:
- features: bfloat16 [6144, 256], P(('col', 'row')), may hold values from -6 to 6
- edge_tiles: bfloat16 [8, 4, 12, 256, 256], P('row', 'col'), may hold values from 0.006225586 to 0.0625
- tile_rows: int32 [8, 4, 12], P('row', 'col'), may hold values from 0 to 2, as said below
- tile_cols: int32 [8, 4, 12], P('row', 'col'), may hold values from 0 to 5
- tile_count: int32 [8, 4], P('row', 'col'), may hold values from 3 to 12, as said below
- weight: bfloat16 [256, 256], replicated, may hold values from -0.375 to 0.375
- cotangent: bfloat16 [6144, 256], P(('row', 'col')), may hold values from -6 to 6
Outputs:
- activated: bfloat16 [6144, 256], P(('row', 'col'))
- feature_grad: bfloat16 [6144, 256], P(('col', 'row'))
The draws below stay inside these ranges and needn't reach their ends.
Inputs may be any that keep to these rules, and one draw needn't show every extreme that they name: Within one device the pairs (tile_rows, tile_cols) of all 12 slots are distinct. Slots at or past tile_count hold no edges of the graph.
All inputs are finite; a program needn't handle non-finite values.
Results may differ from the reference program's by a relative error of at most 0.006.
Values may be sent and summed in bfloat16 or wider, within the bound.
No kernel may reach another device: no remote copies, remote signals or barrier semaphores. Data moves between devices by JAX's collectives and lax.ppermute only.
A program may use at most 64 MiB of HBM per device.

```python
import math
import jax
import jax.numpy as jnp
from jax import lax

FEAT = 256
TILE = 256
ROW_TILES = 3
COL_TILES = 6
SLOTS = 12
NODES = 6144
N_ROW = 8
N_COL = 4


def slot_places(key):
    device_total = N_ROW * N_COL
    keys = jax.random.split(jax.random.fold_in(key, 11), device_total)
    places = jax.vmap(lambda single: jax.random.permutation(single, ROW_TILES * COL_TILES)[:SLOTS])(keys)
    return places.reshape(N_ROW, N_COL, SLOTS).astype(jnp.int32)


def draw_tile_rows(key, part):
    return (slot_places(key) // COL_TILES).astype(jnp.int32)


def draw_tile_cols(key, part):
    return (slot_places(key) % COL_TILES).astype(jnp.int32)


def draw_tile_count(key, part):
    device_total = N_ROW * N_COL
    base_count = jax.random.randint(jax.random.fold_in(key, 5), (device_total,), SLOTS // 4, SLOTS // 2 + 1)
    heavy = jax.random.randint(jax.random.fold_in(key, 6), (device_total,), 0, 8) == 0
    counts = jnp.where(heavy, SLOTS, base_count).astype(jnp.int32)
    chosen = jax.random.randint(jax.random.fold_in(key, 7), (), 0, device_total)
    counts = counts.at[chosen].set(SLOTS)
    counts = counts.at[(chosen + 1) % device_total].set(SLOTS // 4)
    return counts.reshape(N_ROW, N_COL).astype(jnp.int32)


def steps_of(own_key, shape, shards, least, largest):
    gain, own = 1.0, jax.random.fold_in(own_key, 6)
    for dim, parts in shards:
        steps = jnp.exp(jax.random.uniform(jax.random.fold_in(own, dim), (parts,), jnp.float32, least / len(shards), largest / len(shards)))
        gain = gain * jnp.repeat(steps, shape[dim] // parts).reshape([-1 if axis == dim else 1 for axis in range(len(shape))])
    return gain


def gaussian(own_key, shape, width, bound, cuts=(), kind=jnp.bfloat16):
    drawn = width * jax.random.normal(own_key, shape, jnp.float32)
    if cuts:
        drawn = drawn * steps_of(own_key, shape, cuts, -0.22, 0.18)
    return jnp.clip(drawn, -bound, bound).astype(kind)


def setup_inputs(seed: int = 0) -> dict:
    key_of = jax.random.split(jax.random.key(seed), 8)
    features = gaussian(key_of[0], (NODES, FEAT), 1.0, 6.0, ((0, 32),))
    edge_tiles = jnp.clip(jnp.exp(math.log(0.0625) - 2.306499 * jax.random.uniform(key_of[1], (N_ROW, N_COL, SLOTS, TILE, TILE), jnp.float32) ** steps_of(key_of[1], (N_ROW, N_COL, SLOTS, TILE, TILE), ((0, 8), (1, 4)), -0.2, 0.2)), 0.006225586, 0.0625).astype(jnp.bfloat16)
    tile_rows = draw_tile_rows(jax.random.fold_in(key_of[7], 71), 0)
    tile_cols = draw_tile_cols(jax.random.fold_in(key_of[7], 71), 0)
    tile_count = draw_tile_count(jax.random.fold_in(key_of[7], 71), 0)
    weight = gaussian(key_of[5], (FEAT, FEAT), FEAT ** -0.5, 0.375)
    cotangent = gaussian(key_of[6], (NODES, FEAT), 1.0, 6.0, ((0, 32),))
    return dict(features=features, edge_tiles=edge_tiles, tile_rows=tile_rows, tile_cols=tile_cols, tile_count=tile_count, weight=weight, cotangent=cotangent)


def silu_slope(mixed):
    sigma = jax.nn.sigmoid(mixed)
    return sigma * (1.0 + mixed * (1.0 - sigma))


def reference(features, edge_tiles, tile_rows, tile_cols, tile_count, weight, cotangent):
    highest = lax.Precision.HIGHEST
    device_total = N_ROW * N_COL
    flat_tiles = edge_tiles.reshape(device_total, SLOTS, TILE, TILE)
    flat_rows = tile_rows.reshape(device_total, SLOTS)
    flat_cols = tile_cols.reshape(device_total, SLOTS)
    flat_count = tile_count.reshape(device_total)
    numbers = jnp.arange(device_total, dtype=jnp.int32)
    slot_index = jnp.arange(SLOTS, dtype=jnp.int32)
    row_index = jnp.arange(ROW_TILES, dtype=jnp.int32)
    col_index = jnp.arange(COL_TILES, dtype=jnp.int32)
    by_column = features.reshape(N_COL, COL_TILES, TILE, FEAT)

    def forward_step(running, inputs):
        number, blocks, row_slots, col_slots, filled = inputs
        row_block = number // N_COL
        col_block = number % N_COL
        column_rows = lax.dynamic_index_in_dim(by_column, col_block, 0, keepdims=False)
        picked = column_rows[col_slots].astype(jnp.float32)
        products = jnp.einsum("kij,kjf->kif", blocks.astype(jnp.float32), picked, precision=highest)
        occupied = (slot_index < filled).astype(jnp.float32)
        place_rows = (row_slots[None, :] == row_index[:, None]).astype(jnp.float32) * occupied[None, :]
        partial_value = jnp.einsum("rk,kif->rif", place_rows, products, precision=highest)
        current = lax.dynamic_index_in_dim(running, row_block, 0, keepdims=False)
        running = lax.dynamic_update_index_in_dim(running, current + partial_value, row_block, 0)
        return running, None

    start_rows = jnp.zeros((N_ROW, ROW_TILES, TILE, FEAT), jnp.float32)
    summed = lax.scan(forward_step, start_rows, (numbers, flat_tiles, flat_rows, flat_cols, flat_count))[0]
    aggregated = summed.reshape(NODES, FEAT).astype(jnp.bfloat16)
    mixed = jnp.dot(aggregated, weight, preferred_element_type=jnp.float32)
    activated = jax.nn.silu(mixed).astype(jnp.bfloat16)
    scaled = (cotangent.astype(jnp.float32) * silu_slope(mixed)).astype(jnp.bfloat16)
    pulled = jnp.dot(scaled, weight.T, preferred_element_type=jnp.float32).astype(jnp.bfloat16)
    by_row = pulled.reshape(N_ROW, ROW_TILES, TILE, FEAT)

    def backward_step(running, inputs):
        number, blocks, row_slots, col_slots, filled = inputs
        row_block = number // N_COL
        col_block = number % N_COL
        block_rows = lax.dynamic_index_in_dim(by_row, row_block, 0, keepdims=False)
        chosen = block_rows[row_slots].astype(jnp.float32)
        flipped = jnp.einsum("kij,kif->kjf", blocks.astype(jnp.float32), chosen, precision=highest)
        occupied = (slot_index < filled).astype(jnp.float32)
        place_cols = (col_slots[None, :] == col_index[:, None]).astype(jnp.float32) * occupied[None, :]
        partial_value = jnp.einsum("ck,kjf->cjf", place_cols, flipped, precision=highest)
        current = lax.dynamic_index_in_dim(running, col_block, 0, keepdims=False)
        running = lax.dynamic_update_index_in_dim(running, current + partial_value, col_block, 0)
        return running, None

    start_cols = jnp.zeros((N_COL, COL_TILES, TILE, FEAT), jnp.float32)
    grads = lax.scan(backward_step, start_cols, (numbers, flat_tiles, flat_rows, flat_cols, flat_count))[0]
    feature_grad = grads.reshape(NODES, FEAT).astype(jnp.bfloat16)
    return (activated, feature_grad)
```

```python
import jax
import jax.numpy as jnp
from jax import lax
from jax.sharding import PartitionSpec as P


def silu_slope(mixed):
    sigma = jax.nn.sigmoid(mixed)
    return sigma * (1.0 + mixed * (1.0 - sigma))


def dense_layer(summed, grad_rows, weight):
    aggregated = summed.astype(jnp.bfloat16)
    mixed = jnp.dot(aggregated, weight, preferred_element_type=jnp.float32)
    activated = jax.nn.silu(mixed).astype(jnp.bfloat16)
    scaled = (grad_rows.astype(jnp.float32) * silu_slope(mixed)).astype(jnp.bfloat16)
    pulled = jnp.dot(scaled, weight.T, preferred_element_type=jnp.float32).astype(jnp.bfloat16)
    return (activated, pulled)


def scatter_sum(partial, axis):
    n = lax.axis_size(axis)
    me = lax.axis_index(axis)
    chunks = partial.reshape(n, partial.shape[0] // n, partial.shape[1])
    sent = chunks.astype(jnp.bfloat16)
    total = lax.dynamic_index_in_dim(chunks, me, 0, keepdims=False)
    for shift in range(1, n):
        piece = lax.dynamic_index_in_dim(sent, (me + shift) % n, 0, keepdims=False)
        got = lax.ppermute(piece, axis, [(i, (i + shift) % n) for i in range(n)])
        total = total + got.astype(jnp.float32)
    return total


def gather_rows(rows, axis):
    n = lax.axis_size(axis)
    me = lax.axis_index(axis)
    out = jnp.zeros((n,) + rows.shape, rows.dtype)
    out = lax.dynamic_update_index_in_dim(out, rows, me, 0)
    for shift in range(1, n):
        got = lax.ppermute(rows, axis, [(i, (i + shift) % n) for i in range(n)])
        out = lax.dynamic_update_index_in_dim(out, got, (me - shift) % n, 0)
    return out.reshape(n * rows.shape[0], rows.shape[1])


def on_device(features, edge_tiles, tile_rows, tile_cols, tile_count, weight, cotangent):
    blocks = edge_tiles[0, 0]
    row_slots = tile_rows[0, 0]
    col_slots = tile_cols[0, 0]
    filled = tile_count[0, 0]
    slot_total = blocks.shape[0]
    tile_size = blocks.shape[1]
    feat_width = features.shape[1]
    own_rows = features.shape[0]
    row_tiles = own_rows * lax.axis_size("col") // tile_size
    col_tiles = own_rows * lax.axis_size("row") // tile_size
    occupied = (jnp.arange(slot_total, dtype=jnp.int32) < filled).astype(jnp.bfloat16)
    row_hot = (row_slots[None, :] == jnp.arange(row_tiles, dtype=jnp.int32)[:, None]).astype(jnp.bfloat16)
    col_hot = (col_slots[None, :] == jnp.arange(col_tiles, dtype=jnp.int32)[:, None]).astype(jnp.bfloat16)
    select = row_hot[:, None, :] * col_hot[None, :, :] * occupied[None, None, :]
    dense = jnp.einsum("tck,kij->ticj", select, blocks, preferred_element_type=jnp.float32)
    dense = dense.astype(jnp.bfloat16).reshape(row_tiles * tile_size, col_tiles * tile_size)

    gathered = lax.all_gather(features, "row", axis=0, tiled=True)
    partial_value = jnp.dot(dense, gathered, preferred_element_type=jnp.float32)
    own_sums = scatter_sum(partial_value, "col")
    activated, pulled_own = dense_layer(own_sums, cotangent, weight)
    pulled_block = gather_rows(pulled_own, "col")
    partial_grad = lax.dot_general(
        dense, pulled_block, (((0,), (0,)), ((), ())), preferred_element_type=jnp.float32
    )
    feature_grad = scatter_sum(partial_grad, "row").astype(jnp.bfloat16)
    return (activated, feature_grad)


def solution(mesh):
    return jax.shard_map(
        on_device,
        mesh=mesh,
        in_specs=(
            P(("col", "row"), None),
            P("row", "col", None, None, None),
            P("row", "col", None),
            P("row", "col", None),
            P("row", "col"),
            P(),
            P(("row", "col"), None),
        ),
        out_specs=(P(("row", "col"), None), P(("col", "row"), None)),
        check_vma=False,
    )
```

```python
import jax
import jax.numpy as jnp
from jax import lax
from jax.experimental import pallas as pl
from jax.experimental.pallas import tpu as pltpu
from jax.sharding import PartitionSpec as P


def silu_slope(mixed):
    sigma = jax.nn.sigmoid(mixed)
    return sigma * (1.0 + mixed * (1.0 - sigma))


def dense_layer(summed, grad_rows, weight):
    aggregated = summed.astype(jnp.bfloat16)
    mixed = jnp.dot(aggregated, weight, preferred_element_type=jnp.float32)
    activated = jax.nn.silu(mixed).astype(jnp.bfloat16)
    scaled = (grad_rows.astype(jnp.float32) * silu_slope(mixed)).astype(jnp.bfloat16)
    pulled = jnp.dot(scaled, weight.T, preferred_element_type=jnp.float32).astype(jnp.bfloat16)
    return (activated, pulled)


def split_out(acc_ref, own_ref, send_ref, me):
    chunk = own_ref.shape[0]
    n = send_ref.shape[0] + 1
    own_ref[...] = acc_ref[pl.ds(pl.multiple_of(me * chunk, 8), chunk), :]
    for shift in range(1, n):
        start = pl.multiple_of(((me + shift) % n) * chunk, 8)
        send_ref[shift - 1] = acc_ref[pl.ds(start, chunk), :].astype(send_ref.dtype)


def forward_kernel(rows_ref, cols_ref, info_ref, a_ref, f_ref, own_ref, send_ref, acc_ref):
    tile = a_ref.shape[1]
    acc_ref[...] = jnp.zeros_like(acc_ref)

    def step(k, carry):
        f = f_ref[pl.ds(pl.multiple_of(cols_ref[k] * tile, tile), tile), :]
        rows = pl.ds(pl.multiple_of(rows_ref[k] * tile, tile), tile)
        acc_ref[rows, :] += jnp.dot(a_ref[k], f, preferred_element_type=jnp.float32)
        return carry

    lax.fori_loop(0, jnp.minimum(info_ref[0], a_ref.shape[0]), step, 0)
    split_out(acc_ref, own_ref, send_ref, info_ref[1])


def backward_kernel(rows_ref, cols_ref, info_ref, a_ref, mine_ref, *rest):
    got_refs = rest[:-4]
    own_ref, send_ref, block_ref, acc_ref = rest[-4:]
    tile = a_ref.shape[1]
    chunk = mine_ref.shape[0]
    n = len(got_refs) + 1
    me = info_ref[1]
    block_ref[pl.ds(pl.multiple_of(me * chunk, 16), chunk), :] = mine_ref[...]
    for shift in range(1, n):
        start = pl.multiple_of(((me - shift + n) % n) * chunk, 16)
        block_ref[pl.ds(start, chunk), :] = got_refs[shift - 1][...]
    acc_ref[...] = jnp.zeros_like(acc_ref)

    def step(k, carry):
        p = block_ref[pl.ds(pl.multiple_of(rows_ref[k] * tile, tile), tile), :]
        cols = pl.ds(pl.multiple_of(cols_ref[k] * tile, tile), tile)
        acc_ref[cols, :] += lax.dot_general(
            a_ref[k], p, (((0,), (0,)), ((), ())), preferred_element_type=jnp.float32
        )
        return carry

    lax.fori_loop(0, jnp.minimum(info_ref[0], a_ref.shape[0]), step, 0)
    split_out(acc_ref, own_ref, send_ref, info_ref[2])


SMEM = pl.BlockSpec(memory_space=pltpu.SMEM)
VMEM = pl.BlockSpec(memory_space=pltpu.VMEM)


def tile_products(rows, cols, info, blocks, features, parts):
    out_rows = parts[0] * parts[1]
    chunk = parts[1]
    return pl.pallas_call(
        forward_kernel,
        out_shape=(
            jax.ShapeDtypeStruct((chunk, features.shape[1]), jnp.float32),
            jax.ShapeDtypeStruct((parts[0] - 1, chunk, features.shape[1]), jnp.bfloat16),
        ),
        in_specs=[SMEM, SMEM, SMEM, VMEM, VMEM],
        out_specs=(VMEM, VMEM),
        scratch_shapes=[pltpu.VMEM((out_rows, features.shape[1]), jnp.float32)],
    )(rows, cols, info, blocks, features)


def tile_products_t(rows, cols, info, blocks, mine, got, n_out, out_rows):
    chunk = out_rows // n_out
    width = mine.shape[1]
    return pl.pallas_call(
        backward_kernel,
        out_shape=(
            jax.ShapeDtypeStruct((chunk, width), jnp.float32),
            jax.ShapeDtypeStruct((n_out - 1, chunk, width), jnp.bfloat16),
        ),
        in_specs=[SMEM, SMEM, SMEM, VMEM, VMEM] + [VMEM] * len(got),
        out_specs=(VMEM, VMEM),
        scratch_shapes=[
            pltpu.VMEM(((len(got) + 1) * mine.shape[0], width), jnp.bfloat16),
            pltpu.VMEM((out_rows, width), jnp.float32),
        ],
    )(rows, cols, info, blocks, mine, *got)


def shifts(axis):
    n = lax.axis_size(axis)
    return [[(i, (i + shift) % n) for i in range(n)] for shift in range(1, n)]


def on_device(features, edge_tiles, tile_rows, tile_cols, tile_count, weight, cotangent):
    blocks = edge_tiles[0, 0]
    row_slots = tile_rows[0, 0]
    col_slots = tile_cols[0, 0]
    filled = tile_count[0, 0]
    n_row = lax.axis_size("row")
    n_col = lax.axis_size("col")
    me_row = lax.axis_index("row")
    me_col = lax.axis_index("col")
    own_rows = features.shape[0]

    gathered = lax.all_gather(features, "row", axis=0, tiled=True)
    info = jnp.stack([filled, me_col, me_row]).astype(jnp.int32)
    own, send = tile_products(row_slots, col_slots, info, blocks, gathered, (n_col, own_rows))
    total = own
    for shift, perm in enumerate(shifts("col")):
        total = total + lax.ppermute(send[shift], "col", perm).astype(jnp.float32)
    activated, pulled_own = dense_layer(total, cotangent, weight)
    got = [lax.ppermute(pulled_own, "col", perm) for perm in shifts("col")]
    own_g, send_g = tile_products_t(
        row_slots, col_slots, info, blocks, pulled_own, got, n_row, n_row * own_rows
    )
    total_g = own_g
    for shift, perm in enumerate(shifts("row")):
        total_g = total_g + lax.ppermute(send_g[shift], "row", perm).astype(jnp.float32)
    return (activated, total_g.astype(jnp.bfloat16))


def solution(mesh):
    return jax.shard_map(
        on_device,
        mesh=mesh,
        in_specs=(
            P(("col", "row"), None),
            P("row", "col", None, None, None),
            P("row", "col", None),
            P("row", "col", None),
            P("row", "col"),
            P(),
            P(("row", "col"), None),
        ),
        out_specs=(P(("row", "col"), None), P(("col", "row"), None)),
        check_vma=False,
    )
```

```python
import functools

import jax
import jax.numpy as jnp
from jax import lax
from jax.experimental import pallas as pl
from jax.experimental.pallas import tpu as pltpu
from jax.sharding import PartitionSpec as P


def silu_slope(mixed):
    sigma = jax.nn.sigmoid(mixed)
    return sigma * (1.0 + mixed * (1.0 - sigma))


def dense_layer(summed, grad_rows, weight):
    aggregated = summed.astype(jnp.bfloat16)
    mixed = jnp.dot(aggregated, weight, preferred_element_type=jnp.float32)
    activated = jax.nn.silu(mixed).astype(jnp.bfloat16)
    scaled = (grad_rows.astype(jnp.float32) * silu_slope(mixed)).astype(jnp.bfloat16)
    pulled = jnp.dot(scaled, weight.T, preferred_element_type=jnp.float32).astype(jnp.bfloat16)
    return (activated, pulled)


def split_out(acc_ref, own_ref, send_refs, me):
    chunk = own_ref.shape[0]
    n = len(send_refs) + 1
    own_ref[...] = acc_ref[pl.ds(pl.multiple_of(me * chunk, 8), chunk), :]
    for shift in range(1, n):
        start = pl.multiple_of(((me + shift) % n) * chunk, 8)
        send_refs[shift - 1][...] = acc_ref[pl.ds(start, chunk), :].astype(send_refs[shift - 1].dtype)


def forward_kernel(rows_ref, cols_ref, info_ref, a_ref, f_ref, own_ref, *rest):
    send_refs, acc_ref = rest[:-1], rest[-1]
    tile = a_ref.shape[1]
    acc_ref[...] = jnp.zeros_like(acc_ref)

    def step(k, carry):
        f = f_ref[pl.ds(pl.multiple_of(cols_ref[k] * tile, tile), tile), :]
        rows = pl.ds(pl.multiple_of(rows_ref[k] * tile, tile), tile)
        acc_ref[rows, :] += jnp.dot(a_ref[k], f, preferred_element_type=jnp.float32)
        return carry

    lax.fori_loop(0, jnp.minimum(info_ref[0], a_ref.shape[0]), step, 0)
    split_out(acc_ref, own_ref, send_refs, lax.axis_index("col"))


def backward_kernel(n, rows_ref, cols_ref, info_ref, a_ref, mine_ref, *rest):
    got_refs = rest[: n - 1]
    own_ref = rest[n - 1]
    send_refs = rest[n:-2]
    block_ref, acc_ref = rest[-2:]
    tile = a_ref.shape[1]
    chunk = mine_ref.shape[0]
    me = lax.axis_index("col")
    block_ref[pl.ds(pl.multiple_of(me * chunk, 16), chunk), :] = mine_ref[...]
    for shift in range(1, n):
        start = pl.multiple_of(((me - shift + n) % n) * chunk, 16)
        block_ref[pl.ds(start, chunk), :] = got_refs[shift - 1][...]
    acc_ref[...] = jnp.zeros_like(acc_ref)

    def step(k, carry):
        p = block_ref[pl.ds(pl.multiple_of(rows_ref[k] * tile, tile), tile), :]
        cols = pl.ds(pl.multiple_of(cols_ref[k] * tile, tile), tile)
        acc_ref[cols, :] += lax.dot_general(
            a_ref[k], p, (((0,), (0,)), ((), ())), preferred_element_type=jnp.float32
        )
        return carry

    lax.fori_loop(0, jnp.minimum(info_ref[0], a_ref.shape[0]), step, 0)
    split_out(acc_ref, own_ref, send_refs, lax.axis_index("row"))


SMEM = pl.BlockSpec(memory_space=pltpu.SMEM)
VMEM = pl.BlockSpec(memory_space=pltpu.VMEM)


def tile_products(rows, cols, info, blocks, features, parts):
    out_rows = parts[0] * parts[1]
    chunk = parts[1]
    return pl.pallas_call(
        forward_kernel,
        out_shape=(jax.ShapeDtypeStruct((chunk, features.shape[1]), jnp.float32),)
        + (jax.ShapeDtypeStruct((chunk, features.shape[1]), jnp.bfloat16),) * (parts[0] - 1),
        in_specs=[SMEM, SMEM, SMEM, VMEM, VMEM],
        out_specs=(VMEM,) * parts[0],
        scratch_shapes=[pltpu.VMEM((out_rows, features.shape[1]), jnp.float32)],
    )(rows, cols, info, blocks, features)


def tile_products_t(rows, cols, info, blocks, mine, got, n_out, out_rows):
    chunk = out_rows // n_out
    width = mine.shape[1]
    return pl.pallas_call(
        functools.partial(backward_kernel, len(got) + 1),
        out_shape=(jax.ShapeDtypeStruct((chunk, width), jnp.float32),)
        + (jax.ShapeDtypeStruct((chunk, width), jnp.bfloat16),) * (n_out - 1),
        in_specs=[SMEM, SMEM, SMEM, VMEM, VMEM] + [VMEM] * len(got),
        out_specs=(VMEM,) * n_out,
        scratch_shapes=[
            pltpu.VMEM(((len(got) + 1) * mine.shape[0], width), jnp.bfloat16),
            pltpu.VMEM((out_rows, width), jnp.float32),
        ],
    )(rows, cols, info, blocks, mine, *got)


def shifts(axis):
    n = lax.axis_size(axis)
    return [[(i, (i + shift) % n) for i in range(n)] for shift in range(1, n)]


def on_device(features, edge_tiles, tile_rows, tile_cols, tile_count, weight, cotangent):
    blocks = edge_tiles[0, 0]
    row_slots = tile_rows[0, 0]
    col_slots = tile_cols[0, 0]
    n_row = lax.axis_size("row")
    n_col = lax.axis_size("col")
    own_rows = features.shape[0]

    gathered = lax.all_gather(features, "row", axis=0, tiled=True)
    info = tile_count.reshape(1)
    own, *send = tile_products(row_slots, col_slots, info, blocks, gathered, (n_col, own_rows))
    total = own
    for shift, perm in enumerate(shifts("col")):
        total = total + lax.ppermute(send[shift], "col", perm).astype(jnp.float32)
    activated, pulled_own = dense_layer(total, cotangent, weight)
    got = [lax.ppermute(pulled_own, "col", perm) for perm in shifts("col")]
    own_g, *send_g = tile_products_t(
        row_slots, col_slots, info, blocks, pulled_own, got, n_row, n_row * own_rows
    )
    total_g = own_g
    for shift, perm in enumerate(shifts("row")):
        total_g = total_g + lax.ppermute(send_g[shift], "row", perm).astype(jnp.float32)
    return (activated, total_g.astype(jnp.bfloat16))


def solution(mesh):
    return jax.shard_map(
        on_device,
        mesh=mesh,
        in_specs=(
            P(("col", "row"), None),
            P("row", "col", None, None, None),
            P("row", "col", None),
            P("row", "col", None),
            P("row", "col"),
            P(),
            P(("row", "col"), None),
        ),
        out_specs=(P(("row", "col"), None), P(("col", "row"), None)),
        check_vma=False,
    )
```

```python
import functools

import jax
import jax.numpy as jnp
from jax import lax
from jax.experimental import pallas as pl
from jax.experimental.pallas import tpu as pltpu
from jax.sharding import PartitionSpec as P

SMEM = pl.BlockSpec(memory_space=pltpu.SMEM)
VMEM = pl.BlockSpec(memory_space=pltpu.VMEM)


def silu_slope(mixed):
    sigma = jax.nn.sigmoid(mixed)
    return sigma * (1.0 + mixed * (1.0 - sigma))


def dense_layer(summed, grad_rows, weight):
    aggregated = summed.astype(jnp.bfloat16)
    mixed = jnp.dot(aggregated, weight, preferred_element_type=jnp.float32)
    activated = jax.nn.silu(mixed).astype(jnp.bfloat16)
    scaled = (grad_rows.astype(jnp.float32) * silu_slope(mixed)).astype(jnp.bfloat16)
    pulled = jnp.dot(scaled, weight.T, preferred_element_type=jnp.float32).astype(jnp.bfloat16)
    return (activated, pulled)


def dense_kernel(n, own_ref, *rest):
    got_refs = rest[: n - 1]
    grad_ref, weight_ref, act_ref, pulled_ref = rest[n - 1:]
    total = own_ref[...]
    for got in got_refs:
        total = total + got[...].astype(jnp.float32)
    weight = weight_ref[...]
    mixed = jnp.dot(total.astype(jnp.bfloat16), weight, preferred_element_type=jnp.float32)
    sigma = jax.nn.sigmoid(mixed)
    act_ref[...] = (mixed * sigma).astype(act_ref.dtype)
    slope = sigma * (1.0 + mixed * (1.0 - sigma))
    scaled = (grad_ref[...].astype(jnp.float32) * slope).astype(jnp.bfloat16)
    pulled_ref[...] = lax.dot_general(
        scaled, weight, (((1,), (1,)), ((), ())), preferred_element_type=jnp.float32
    ).astype(pulled_ref.dtype)


def dense_layer_kernel(own, got, grad_rows, weight):
    shape = jax.ShapeDtypeStruct(own.shape, jnp.bfloat16)
    return pl.pallas_call(
        functools.partial(dense_kernel, len(got) + 1),
        out_shape=(shape, shape),
        in_specs=[VMEM] * (len(got) + 3),
        out_specs=(VMEM, VMEM),
    )(own, *got, grad_rows, weight)


def split_out(acc_ref, own_ref, send_refs, me):
    chunk = own_ref.shape[0]
    n = len(send_refs) + 1
    own_ref[...] = acc_ref[pl.ds(pl.multiple_of(me * chunk, 8), chunk), :]
    for shift in range(1, n):
        start = pl.multiple_of(((me + shift) % n) * chunk, 8)
        send_refs[shift - 1][...] = acc_ref[pl.ds(start, chunk), :].astype(send_refs[shift - 1].dtype)


def forward_kernel(rows_ref, cols_ref, info_ref, a_ref, f_ref, own_ref, *rest):
    send_refs, acc_ref = rest[:-1], rest[-1]
    tile = a_ref.shape[1]
    acc_ref[...] = jnp.zeros_like(acc_ref)

    def step(k, carry):
        f = f_ref[pl.ds(pl.multiple_of(cols_ref[k] * tile, tile), tile), :]
        rows = pl.ds(pl.multiple_of(rows_ref[k] * tile, tile), tile)
        acc_ref[rows, :] += jnp.dot(a_ref[k], f, preferred_element_type=jnp.float32)
        return carry

    lax.fori_loop(0, jnp.minimum(info_ref[0], a_ref.shape[0]), step, 0)
    split_out(acc_ref, own_ref, send_refs, lax.axis_index("col"))


def backward_kernel(n, rows_ref, cols_ref, info_ref, a_ref, mine_ref, *rest):
    got_refs = rest[: n - 1]
    own_ref = rest[n - 1]
    send_refs = rest[n:-2]
    block_ref, acc_ref = rest[-2:]
    tile = a_ref.shape[1]
    chunk = mine_ref.shape[0]
    me = lax.axis_index("col")
    block_ref[pl.ds(pl.multiple_of(me * chunk, 16), chunk), :] = mine_ref[...]
    for shift in range(1, n):
        start = pl.multiple_of(((me - shift + n) % n) * chunk, 16)
        block_ref[pl.ds(start, chunk), :] = got_refs[shift - 1][...]
    acc_ref[...] = jnp.zeros_like(acc_ref)

    def step(k, carry):
        p = block_ref[pl.ds(pl.multiple_of(rows_ref[k] * tile, tile), tile), :]
        cols = pl.ds(pl.multiple_of(cols_ref[k] * tile, tile), tile)
        acc_ref[cols, :] += lax.dot_general(
            a_ref[k], p, (((0,), (0,)), ((), ())), preferred_element_type=jnp.float32
        )
        return carry

    lax.fori_loop(0, jnp.minimum(info_ref[0], a_ref.shape[0]), step, 0)
    split_out(acc_ref, own_ref, send_refs, lax.axis_index("row"))


def tile_products(rows, cols, info, blocks, features, parts):
    out_rows = parts[0] * parts[1]
    chunk = parts[1]
    return pl.pallas_call(
        forward_kernel,
        out_shape=(jax.ShapeDtypeStruct((chunk, features.shape[1]), jnp.float32),)
        + (jax.ShapeDtypeStruct((chunk, features.shape[1]), jnp.bfloat16),) * (parts[0] - 1),
        in_specs=[SMEM, SMEM, SMEM, VMEM, VMEM],
        out_specs=(VMEM,) * parts[0],
        scratch_shapes=[pltpu.VMEM((out_rows, features.shape[1]), jnp.float32)],
    )(rows, cols, info, blocks, features)


def tile_products_t(rows, cols, info, blocks, mine, got, n_out, out_rows):
    chunk = out_rows // n_out
    width = mine.shape[1]
    return pl.pallas_call(
        functools.partial(backward_kernel, len(got) + 1),
        out_shape=(jax.ShapeDtypeStruct((chunk, width), jnp.float32),)
        + (jax.ShapeDtypeStruct((chunk, width), jnp.bfloat16),) * (n_out - 1),
        in_specs=[SMEM, SMEM, SMEM, VMEM, VMEM] + [VMEM] * len(got),
        out_specs=(VMEM,) * n_out,
        scratch_shapes=[
            pltpu.VMEM(((len(got) + 1) * mine.shape[0], width), jnp.bfloat16),
            pltpu.VMEM((out_rows, width), jnp.float32),
        ],
    )(rows, cols, info, blocks, mine, *got)


def shifts(axis):
    n = lax.axis_size(axis)
    return [[(i, (i + shift) % n) for i in range(n)] for shift in range(1, n)]


def on_device(features, edge_tiles, tile_rows, tile_cols, tile_count, weight, cotangent):
    blocks = edge_tiles[0, 0]
    row_slots = tile_rows[0, 0]
    col_slots = tile_cols[0, 0]
    n_row = lax.axis_size("row")
    n_col = lax.axis_size("col")
    own_rows = features.shape[0]

    gathered = lax.all_gather(features, "row", axis=0, tiled=True)
    info = tile_count.reshape(1)
    own, *send = tile_products(row_slots, col_slots, info, blocks, gathered, (n_col, own_rows))
    got_f = [lax.ppermute(send[shift], "col", perm) for shift, perm in enumerate(shifts("col"))]
    activated, pulled_own = dense_layer_kernel(own, got_f, cotangent, weight)
    got = [lax.ppermute(pulled_own, "col", perm) for perm in shifts("col")]
    own_g, *send_g = tile_products_t(
        row_slots, col_slots, info, blocks, pulled_own, got, n_row, n_row * own_rows
    )
    total_g = own_g
    for shift, perm in enumerate(shifts("row")):
        total_g = total_g + lax.ppermute(send_g[shift], "row", perm).astype(jnp.float32)
    return (activated, total_g.astype(jnp.bfloat16))


def solution(mesh):
    return jax.shard_map(
        on_device,
        mesh=mesh,
        in_specs=(
            P(("col", "row"), None),
            P("row", "col", None, None, None),
            P("row", "col", None),
            P("row", "col", None),
            P("row", "col"),
            P(),
            P(("row", "col"), None),
        ),
        out_specs=(P(("row", "col"), None), P(("col", "row"), None)),
        check_vma=False,
    )
```

```python
import functools

import jax
import jax.numpy as jnp
from jax import lax
from jax.experimental import pallas as pl
from jax.experimental.pallas import tpu as pltpu
from jax.sharding import PartitionSpec as P


def silu_slope(mixed):
    sigma = jax.nn.sigmoid(mixed)
    return sigma * (1.0 + mixed * (1.0 - sigma))


def dense_layer(summed, grad_rows, weight):
    aggregated = summed.astype(jnp.bfloat16)
    mixed = jnp.dot(aggregated, weight, preferred_element_type=jnp.float32)
    activated = jax.nn.silu(mixed).astype(jnp.bfloat16)
    scaled = (grad_rows.astype(jnp.float32) * silu_slope(mixed)).astype(jnp.bfloat16)
    pulled = jnp.dot(scaled, weight.T, preferred_element_type=jnp.float32).astype(jnp.bfloat16)
    return (activated, pulled)


def split_out(acc_ref, own_ref, send_refs, me):
    chunk = own_ref.shape[0]
    n = len(send_refs) + 1
    own_ref[...] = acc_ref[pl.ds(pl.multiple_of(me * chunk, 8), chunk), :]
    for shift in range(1, n):
        start = pl.multiple_of(((me + shift) % n) * chunk, 8)
        send_refs[shift - 1][...] = acc_ref[pl.ds(start, chunk), :].astype(send_refs[shift - 1].dtype)


def forward_kernel(rows_ref, cols_ref, info_ref, a_ref, near_ref, far_ref, own_ref, *rest):
    send_refs, f_ref, acc_ref = rest[:-2], rest[-2], rest[-1]
    tile = a_ref.shape[1]
    chips, piece = near_ref.shape[0], near_ref.shape[1]
    me = lax.axis_index("row")
    core, chip = me % 2, me // 2
    for shift in range(chips):
        owner = (chip - shift + chips) % chips
        near = pl.multiple_of((owner * 2 + core) * piece, 16)
        far = pl.multiple_of((owner * 2 + 1 - core) * piece, 16)
        f_ref[pl.ds(near, piece), :] = near_ref[shift]
        f_ref[pl.ds(far, piece), :] = far_ref[shift]
    acc_ref[...] = jnp.zeros_like(acc_ref)

    def step(k, carry):
        f = f_ref[pl.ds(pl.multiple_of(cols_ref[k] * tile, tile), tile), :]
        rows = pl.ds(pl.multiple_of(rows_ref[k] * tile, tile), tile)
        acc_ref[rows, :] += jnp.dot(a_ref[k], f, preferred_element_type=jnp.float32)
        return carry

    lax.fori_loop(0, jnp.minimum(info_ref[0], a_ref.shape[0]), step, 0)
    split_out(acc_ref, own_ref, send_refs, lax.axis_index("col"))


def backward_kernel(n, rows_ref, cols_ref, info_ref, a_ref, mine_ref, *rest):
    got_refs = rest[: n - 1]
    near_ref, far_ref, block_ref, acc_ref = rest[n - 1:]
    tile = a_ref.shape[1]
    chunk = mine_ref.shape[0]
    me = lax.axis_index("col")
    block_ref[pl.ds(pl.multiple_of(me * chunk, 16), chunk), :] = mine_ref[...]
    for shift in range(1, n):
        start = pl.multiple_of(((me - shift + n) % n) * chunk, 16)
        block_ref[pl.ds(start, chunk), :] = got_refs[shift - 1][...]
    acc_ref[...] = jnp.zeros_like(acc_ref)

    def step(k, carry):
        p = block_ref[pl.ds(pl.multiple_of(rows_ref[k] * tile, tile), tile), :]
        cols = pl.ds(pl.multiple_of(cols_ref[k] * tile, tile), tile)
        acc_ref[cols, :] += lax.dot_general(
            a_ref[k], p, (((0,), (0,)), ((), ())), preferred_element_type=jnp.float32
        )
        return carry

    lax.fori_loop(0, jnp.minimum(info_ref[0], a_ref.shape[0]), step, 0)
    chips = near_ref.shape[0]
    piece = near_ref.shape[1]
    me_row = lax.axis_index("row")
    core, chip = me_row % 2, me_row // 2
    for shift in range(chips):
        owner = (chip + shift) % chips
        near_ref[shift] = acc_ref[pl.ds(pl.multiple_of((owner * 2 + core) * piece, 8), piece), :]
        far_ref[shift] = acc_ref[pl.ds(pl.multiple_of((owner * 2 + 1 - core) * piece, 8), piece), :]


SMEM = pl.BlockSpec(memory_space=pltpu.SMEM)
VMEM = pl.BlockSpec(memory_space=pltpu.VMEM)


def tile_products(rows, cols, info, blocks, near, far, parts):
    out_rows = parts[0] * parts[1]
    chunk = parts[1]
    width = near.shape[2]
    return pl.pallas_call(
        forward_kernel,
        out_shape=(jax.ShapeDtypeStruct((chunk, width), jnp.float32),)
        + (jax.ShapeDtypeStruct((chunk, width), jnp.bfloat16),) * (parts[0] - 1),
        in_specs=[SMEM, SMEM, SMEM, VMEM, VMEM, VMEM],
        out_specs=(VMEM,) * parts[0],
        scratch_shapes=[
            pltpu.VMEM((2 * near.shape[0] * near.shape[1], width), jnp.bfloat16),
            pltpu.VMEM((out_rows, width), jnp.float32),
        ],
    )(rows, cols, info, blocks, near, far)


def tile_products_t(rows, cols, info, blocks, mine, got, n_out, out_rows):
    chunk = out_rows // n_out
    width = mine.shape[1]
    stack = jax.ShapeDtypeStruct((n_out // 2, chunk, width), jnp.float32)
    return pl.pallas_call(
        functools.partial(backward_kernel, len(got) + 1),
        out_shape=(stack, stack),
        in_specs=[SMEM, SMEM, SMEM, VMEM, VMEM] + [VMEM] * len(got),
        out_specs=(VMEM, VMEM),
        scratch_shapes=[
            pltpu.VMEM(((len(got) + 1) * mine.shape[0], width), jnp.bfloat16),
            pltpu.VMEM((out_rows, width), jnp.float32),
        ],
    )(rows, cols, info, blocks, mine, *got)


def shifts(axis):
    n = lax.axis_size(axis)
    return [[(i, (i + shift) % n) for i in range(n)] for shift in range(1, n)]


def chip_shifts(n):
    chips = n // 2
    return [[(i, ((i // 2 + shift) % chips) * 2 + i % 2) for i in range(n)] for shift in range(1, chips)]


def partner(n):
    return [(i, i ^ 1) for i in range(n)]


def on_device(features, edge_tiles, tile_rows, tile_cols, tile_count, weight, cotangent):
    blocks = edge_tiles[0, 0]
    row_slots = tile_rows[0, 0]
    col_slots = tile_cols[0, 0]
    n_row = lax.axis_size("row")
    n_col = lax.axis_size("col")
    own_rows = features.shape[0]

    near = jnp.stack([features] + [lax.ppermute(features, "row", perm) for perm in chip_shifts(n_row)])
    far = lax.ppermute(near, "row", partner(n_row))
    info = tile_count.reshape(1)
    own, *send = tile_products(row_slots, col_slots, info, blocks, near, far, (n_col, own_rows))
    total = own
    for shift, perm in enumerate(shifts("col")):
        total = total + lax.ppermute(send[shift], "col", perm).astype(jnp.float32)
    activated, pulled_own = dense_layer(total, cotangent, weight)
    got = [lax.ppermute(pulled_own, "col", perm) for perm in shifts("col")]
    near_g, far_g = tile_products_t(
        row_slots, col_slots, info, blocks, pulled_own, got, n_row, n_row * own_rows
    )
    chip_sums = near_g + lax.ppermute(far_g, "row", partner(n_row))
    total_g = chip_sums[0]
    for shift, perm in enumerate(chip_shifts(n_row)):
        piece = chip_sums[shift + 1].astype(jnp.bfloat16)
        total_g = total_g + lax.ppermute(piece, "row", perm).astype(jnp.float32)
    return (activated, total_g.astype(jnp.bfloat16))


def solution(mesh):
    return jax.shard_map(
        on_device,
        mesh=mesh,
        in_specs=(
            P(("col", "row"), None),
            P("row", "col", None, None, None),
            P("row", "col", None),
            P("row", "col", None),
            P("row", "col"),
            P(),
            P(("row", "col"), None),
        ),
        out_specs=(P(("row", "col"), None), P(("col", "row"), None)),
        check_vma=False,
    )
```

```python
import functools

import jax
import jax.numpy as jnp
from jax import lax
from jax.experimental import pallas as pl
from jax.experimental.pallas import tpu as pltpu
from jax.sharding import PartitionSpec as P

SMEM = pl.BlockSpec(memory_space=pltpu.SMEM)
VMEM = pl.BlockSpec(memory_space=pltpu.VMEM)
ANY = pl.BlockSpec(memory_space=pl.ANY)


def silu_slope(mixed):
    sigma = jax.nn.sigmoid(mixed)
    return sigma * (1.0 + mixed * (1.0 - sigma))


def dense_layer(summed, grad_rows, weight):
    aggregated = summed.astype(jnp.bfloat16)
    mixed = jnp.dot(aggregated, weight, preferred_element_type=jnp.float32)
    activated = jax.nn.silu(mixed).astype(jnp.bfloat16)
    scaled = (grad_rows.astype(jnp.float32) * silu_slope(mixed)).astype(jnp.bfloat16)
    pulled = jnp.dot(scaled, weight.T, preferred_element_type=jnp.float32).astype(jnp.bfloat16)
    return (activated, pulled)


def split_out(acc_ref, own_ref, send_refs, me):
    chunk = own_ref.shape[0]
    n = len(send_refs) + 1
    own_ref[...] = acc_ref[pl.ds(pl.multiple_of(me * chunk, 8), chunk), :]
    for shift in range(1, n):
        start = pl.multiple_of(((me + shift) % n) * chunk, 8)
        send_refs[shift - 1][...] = acc_ref[pl.ds(start, chunk), :].astype(send_refs[shift - 1].dtype)


def start_tiles(a_hbm, a_vmem, sems, count):
    def begin(k, carry):
        pltpu.make_async_copy(a_hbm.at[k], a_vmem.at[k], sems.at[k]).start()
        return carry

    lax.fori_loop(0, count, begin, 0)


def wait_tile(a_hbm, a_vmem, sems, k):
    pltpu.make_async_copy(a_hbm.at[k], a_vmem.at[k], sems.at[k]).wait()


def forward_kernel(rows_ref, cols_ref, info_ref, a_hbm, near_hbm, far_hbm, own_ref, *rest):
    send_refs = rest[:-5]
    a_vmem, f_ref, acc_ref, tile_sems, piece_sems = rest[-5:]
    slots, tile = a_hbm.shape[0], a_hbm.shape[1]
    chips, piece = near_hbm.shape[0], near_hbm.shape[1]
    me = lax.axis_index("row")
    core, chip = me % 2, me // 2
    pieces = []
    for shift in range(chips):
        owner = (chip - shift + chips) % chips
        for side, src in ((core, near_hbm), (1 - core, far_hbm)):
            dst = f_ref.at[pl.ds(pl.multiple_of((owner * 2 + side) * piece, 16), piece)]
            copy = pltpu.make_async_copy(src.at[shift], dst, piece_sems.at[len(pieces)])
            copy.start()
            pieces.append(copy)
    count = jnp.minimum(info_ref[0], slots)
    start_tiles(a_hbm, a_vmem, tile_sems, count)
    acc_ref[...] = jnp.zeros_like(acc_ref)
    for copy in pieces:
        copy.wait()

    def step(k, carry):
        wait_tile(a_hbm, a_vmem, tile_sems, k)
        f = f_ref[pl.ds(pl.multiple_of(cols_ref[k] * tile, tile), tile), :]
        rows = pl.ds(pl.multiple_of(rows_ref[k] * tile, tile), tile)
        acc_ref[rows, :] += jnp.dot(a_vmem[k], f, preferred_element_type=jnp.float32)
        return carry

    lax.fori_loop(0, count, step, 0)
    split_out(acc_ref, own_ref, send_refs, lax.axis_index("col"))


def backward_kernel(n, rows_ref, cols_ref, info_ref, a_hbm, mine_hbm, *rest):
    got_hbm = rest[: n - 1]
    near_ref, far_ref, a_vmem, block_ref, acc_ref, tile_sems, piece_sems = rest[n - 1:]
    slots, tile = a_hbm.shape[0], a_hbm.shape[1]
    chunk = mine_hbm.shape[0]
    me = lax.axis_index("col")
    pieces = []
    for shift, src in enumerate((mine_hbm,) + tuple(got_hbm)):
        dst = block_ref.at[pl.ds(pl.multiple_of(((me - shift + n) % n) * chunk, 16), chunk)]
        copy = pltpu.make_async_copy(src, dst, piece_sems.at[shift])
        copy.start()
        pieces.append(copy)
    count = jnp.minimum(info_ref[0], slots)
    start_tiles(a_hbm, a_vmem, tile_sems, count)
    acc_ref[...] = jnp.zeros_like(acc_ref)
    for copy in pieces:
        copy.wait()

    def step(k, carry):
        wait_tile(a_hbm, a_vmem, tile_sems, k)
        p = block_ref[pl.ds(pl.multiple_of(rows_ref[k] * tile, tile), tile), :]
        cols = pl.ds(pl.multiple_of(cols_ref[k] * tile, tile), tile)
        acc_ref[cols, :] += lax.dot_general(
            a_vmem[k], p, (((0,), (0,)), ((), ())), preferred_element_type=jnp.float32
        )
        return carry

    lax.fori_loop(0, count, step, 0)
    chips = near_ref.shape[0]
    piece = near_ref.shape[1]
    me_row = lax.axis_index("row")
    core, chip = me_row % 2, me_row // 2
    for shift in range(chips):
        owner = (chip + shift) % chips
        near_ref[shift] = acc_ref[pl.ds(pl.multiple_of((owner * 2 + core) * piece, 8), piece), :]
        far_ref[shift] = acc_ref[pl.ds(pl.multiple_of((owner * 2 + 1 - core) * piece, 8), piece), :]


def tile_products(rows, cols, info, blocks, near, far, parts):
    out_rows = parts[0] * parts[1]
    chunk = parts[1]
    width = near.shape[2]
    return pl.pallas_call(
        forward_kernel,
        out_shape=(jax.ShapeDtypeStruct((chunk, width), jnp.float32),)
        + (jax.ShapeDtypeStruct((chunk, width), jnp.bfloat16),) * (parts[0] - 1),
        in_specs=[SMEM, SMEM, SMEM, ANY, ANY, ANY],
        out_specs=(VMEM,) * parts[0],
        scratch_shapes=[
            pltpu.VMEM(blocks.shape, blocks.dtype),
            pltpu.VMEM((2 * near.shape[0] * near.shape[1], width), jnp.bfloat16),
            pltpu.VMEM((out_rows, width), jnp.float32),
            pltpu.SemaphoreType.DMA((blocks.shape[0],)),
            pltpu.SemaphoreType.DMA((2 * near.shape[0],)),
        ],
    )(rows, cols, info, blocks, near, far)


def tile_products_t(rows, cols, info, blocks, mine, got, n_out, out_rows):
    chunk = out_rows // n_out
    width = mine.shape[1]
    stack = jax.ShapeDtypeStruct((n_out // 2, chunk, width), jnp.float32)
    return pl.pallas_call(
        functools.partial(backward_kernel, len(got) + 1),
        out_shape=(stack, stack),
        in_specs=[SMEM, SMEM, SMEM, ANY, ANY] + [ANY] * len(got),
        out_specs=(VMEM, VMEM),
        scratch_shapes=[
            pltpu.VMEM(blocks.shape, blocks.dtype),
            pltpu.VMEM(((len(got) + 1) * mine.shape[0], width), jnp.bfloat16),
            pltpu.VMEM((out_rows, width), jnp.float32),
            pltpu.SemaphoreType.DMA((blocks.shape[0],)),
            pltpu.SemaphoreType.DMA((len(got) + 1,)),
        ],
    )(rows, cols, info, blocks, mine, *got)


def shifts(axis):
    n = lax.axis_size(axis)
    return [[(i, (i + shift) % n) for i in range(n)] for shift in range(1, n)]


def chip_shifts(n):
    chips = n // 2
    return [[(i, ((i // 2 + shift) % chips) * 2 + i % 2) for i in range(n)] for shift in range(1, chips)]


def partner(n):
    return [(i, i ^ 1) for i in range(n)]


def on_device(features, edge_tiles, tile_rows, tile_cols, tile_count, weight, cotangent):
    blocks = edge_tiles[0, 0]
    row_slots = tile_rows[0, 0]
    col_slots = tile_cols[0, 0]
    n_row = lax.axis_size("row")
    n_col = lax.axis_size("col")
    own_rows = features.shape[0]

    near = jnp.stack([features] + [lax.ppermute(features, "row", perm) for perm in chip_shifts(n_row)])
    far = lax.ppermute(near, "row", partner(n_row))
    info = tile_count.reshape(1)
    own, *send = tile_products(row_slots, col_slots, info, blocks, near, far, (n_col, own_rows))
    total = own
    for shift, perm in enumerate(shifts("col")):
        total = total + lax.ppermute(send[shift], "col", perm).astype(jnp.float32)
    activated, pulled_own = dense_layer(total, cotangent, weight)
    got = [lax.ppermute(pulled_own, "col", perm) for perm in shifts("col")]
    near_g, far_g = tile_products_t(
        row_slots, col_slots, info, blocks, pulled_own, got, n_row, n_row * own_rows
    )
    chip_sums = near_g + lax.ppermute(far_g, "row", partner(n_row))
    total_g = chip_sums[0]
    for shift, perm in enumerate(chip_shifts(n_row)):
        piece = chip_sums[shift + 1].astype(jnp.bfloat16)
        total_g = total_g + lax.ppermute(piece, "row", perm).astype(jnp.float32)
    return (activated, total_g.astype(jnp.bfloat16))


def solution(mesh):
    return jax.shard_map(
        on_device,
        mesh=mesh,
        in_specs=(
            P(("col", "row"), None),
            P("row", "col", None, None, None),
            P("row", "col", None),
            P("row", "col", None),
            P("row", "col"),
            P(),
            P(("row", "col"), None),
        ),
        out_specs=(P(("row", "col"), None), P(("col", "row"), None)),
        check_vma=False,
    )
```

```python
import functools

import jax
import jax.numpy as jnp
from jax import lax
from jax.experimental import pallas as pl
from jax.experimental.pallas import tpu as pltpu
from jax.sharding import PartitionSpec as P


def silu_slope(mixed):
    sigma = jax.nn.sigmoid(mixed)
    return sigma * (1.0 + mixed * (1.0 - sigma))


def dense_layer(summed, grad_rows, weight):
    aggregated = summed.astype(jnp.bfloat16)
    mixed = jnp.dot(aggregated, weight, preferred_element_type=jnp.float32)
    activated = jax.nn.silu(mixed).astype(jnp.bfloat16)
    scaled = (grad_rows.astype(jnp.float32) * silu_slope(mixed)).astype(jnp.bfloat16)
    pulled = jnp.dot(scaled, weight.T, preferred_element_type=jnp.float32).astype(jnp.bfloat16)
    return (activated, pulled)


UNROLL = 4


def run_slots(count, product, place):
    def group(g, carry):
        base = g * UNROLL
        values = [product(base + j) for j in range(UNROLL)]
        for j, value in enumerate(values):
            place(base + j, value)
        return carry

    def single(k, carry):
        place(k, product(k))
        return carry

    lax.fori_loop(0, count // UNROLL, group, 0)
    lax.fori_loop((count // UNROLL) * UNROLL, count, single, 0)


def split_out(acc_ref, own_ref, send_refs, me):
    chunk = own_ref.shape[0]
    n = len(send_refs) + 1
    own_ref[...] = acc_ref[pl.ds(pl.multiple_of(me * chunk, 8), chunk), :]
    for shift in range(1, n):
        start = pl.multiple_of(((me + shift) % n) * chunk, 8)
        send_refs[shift - 1][...] = acc_ref[pl.ds(start, chunk), :].astype(send_refs[shift - 1].dtype)


def forward_kernel(rows_ref, cols_ref, info_ref, a_ref, near_ref, far_ref, own_ref, *rest):
    send_refs, f_ref, acc_ref = rest[:-2], rest[-2], rest[-1]
    tile = a_ref.shape[1]
    chips, piece = near_ref.shape[0], near_ref.shape[1]
    me = lax.axis_index("row")
    core, chip = me % 2, me // 2
    for shift in range(chips):
        owner = (chip - shift + chips) % chips
        near = pl.multiple_of((owner * 2 + core) * piece, 16)
        far = pl.multiple_of((owner * 2 + 1 - core) * piece, 16)
        f_ref[pl.ds(near, piece), :] = near_ref[shift]
        f_ref[pl.ds(far, piece), :] = far_ref[shift]
    acc_ref[...] = jnp.zeros_like(acc_ref)

    def product(k):
        f = f_ref[pl.ds(pl.multiple_of(cols_ref[k] * tile, tile), tile), :]
        return jnp.dot(a_ref[k], f, preferred_element_type=jnp.float32)

    def place(k, value):
        rows = pl.ds(pl.multiple_of(rows_ref[k] * tile, tile), tile)
        acc_ref[rows, :] += value

    run_slots(jnp.minimum(info_ref[0], a_ref.shape[0]), product, place)
    split_out(acc_ref, own_ref, send_refs, lax.axis_index("col"))


def backward_kernel(n, rows_ref, cols_ref, info_ref, a_ref, mine_ref, *rest):
    got_refs = rest[: n - 1]
    near_ref, far_ref, block_ref, acc_ref = rest[n - 1:]
    tile = a_ref.shape[1]
    chunk = mine_ref.shape[0]
    me = lax.axis_index("col")
    block_ref[pl.ds(pl.multiple_of(me * chunk, 16), chunk), :] = mine_ref[...]
    for shift in range(1, n):
        start = pl.multiple_of(((me - shift + n) % n) * chunk, 16)
        block_ref[pl.ds(start, chunk), :] = got_refs[shift - 1][...]
    acc_ref[...] = jnp.zeros_like(acc_ref)

    def product(k):
        p = block_ref[pl.ds(pl.multiple_of(rows_ref[k] * tile, tile), tile), :]
        return lax.dot_general(
            a_ref[k], p, (((0,), (0,)), ((), ())), preferred_element_type=jnp.float32
        )

    def place(k, value):
        cols = pl.ds(pl.multiple_of(cols_ref[k] * tile, tile), tile)
        acc_ref[cols, :] += value

    run_slots(jnp.minimum(info_ref[0], a_ref.shape[0]), product, place)
    chips = near_ref.shape[0]
    piece = near_ref.shape[1]
    me_row = lax.axis_index("row")
    core, chip = me_row % 2, me_row // 2
    for shift in range(chips):
        owner = (chip + shift) % chips
        near_ref[shift] = acc_ref[pl.ds(pl.multiple_of((owner * 2 + core) * piece, 8), piece), :]
        far_ref[shift] = acc_ref[pl.ds(pl.multiple_of((owner * 2 + 1 - core) * piece, 8), piece), :]


SMEM = pl.BlockSpec(memory_space=pltpu.SMEM)
VMEM = pl.BlockSpec(memory_space=pltpu.VMEM)


def tile_products(rows, cols, info, blocks, near, far, parts):
    out_rows = parts[0] * parts[1]
    chunk = parts[1]
    width = near.shape[2]
    return pl.pallas_call(
        forward_kernel,
        out_shape=(jax.ShapeDtypeStruct((chunk, width), jnp.float32),)
        + (jax.ShapeDtypeStruct((chunk, width), jnp.bfloat16),) * (parts[0] - 1),
        in_specs=[SMEM, SMEM, SMEM, VMEM, VMEM, VMEM],
        out_specs=(VMEM,) * parts[0],
        scratch_shapes=[
            pltpu.VMEM((2 * near.shape[0] * near.shape[1], width), jnp.bfloat16),
            pltpu.VMEM((out_rows, width), jnp.float32),
        ],
    )(rows, cols, info, blocks, near, far)


def tile_products_t(rows, cols, info, blocks, mine, got, n_out, out_rows):
    chunk = out_rows // n_out
    width = mine.shape[1]
    stack = jax.ShapeDtypeStruct((n_out // 2, chunk, width), jnp.float32)
    return pl.pallas_call(
        functools.partial(backward_kernel, len(got) + 1),
        out_shape=(stack, stack),
        in_specs=[SMEM, SMEM, SMEM, VMEM, VMEM] + [VMEM] * len(got),
        out_specs=(VMEM, VMEM),
        scratch_shapes=[
            pltpu.VMEM(((len(got) + 1) * mine.shape[0], width), jnp.bfloat16),
            pltpu.VMEM((out_rows, width), jnp.float32),
        ],
    )(rows, cols, info, blocks, mine, *got)


def shifts(axis):
    n = lax.axis_size(axis)
    return [[(i, (i + shift) % n) for i in range(n)] for shift in range(1, n)]


def chip_shifts(n):
    chips = n // 2
    return [[(i, ((i // 2 + shift) % chips) * 2 + i % 2) for i in range(n)] for shift in range(1, chips)]


def partner(n):
    return [(i, i ^ 1) for i in range(n)]


def on_device(features, edge_tiles, tile_rows, tile_cols, tile_count, weight, cotangent):
    blocks = edge_tiles[0, 0]
    row_slots = tile_rows[0, 0]
    col_slots = tile_cols[0, 0]
    n_row = lax.axis_size("row")
    n_col = lax.axis_size("col")
    own_rows = features.shape[0]

    near = jnp.stack([features] + [lax.ppermute(features, "row", perm) for perm in chip_shifts(n_row)])
    far = lax.ppermute(near, "row", partner(n_row))
    info = tile_count.reshape(1)
    own, *send = tile_products(row_slots, col_slots, info, blocks, near, far, (n_col, own_rows))
    total = own
    for shift, perm in enumerate(shifts("col")):
        total = total + lax.ppermute(send[shift], "col", perm).astype(jnp.float32)
    activated, pulled_own = dense_layer(total, cotangent, weight)
    got = [lax.ppermute(pulled_own, "col", perm) for perm in shifts("col")]
    near_g, far_g = tile_products_t(
        row_slots, col_slots, info, blocks, pulled_own, got, n_row, n_row * own_rows
    )
    chip_sums = near_g + lax.ppermute(far_g, "row", partner(n_row))
    total_g = chip_sums[0]
    for shift, perm in enumerate(chip_shifts(n_row)):
        piece = chip_sums[shift + 1].astype(jnp.bfloat16)
        total_g = total_g + lax.ppermute(piece, "row", perm).astype(jnp.float32)
    return (activated, total_g.astype(jnp.bfloat16))


def solution(mesh):
    return jax.shard_map(
        on_device,
        mesh=mesh,
        in_specs=(
            P(("col", "row"), None),
            P("row", "col", None, None, None),
            P("row", "col", None),
            P("row", "col", None),
            P("row", "col"),
            P(),
            P(("row", "col"), None),
        ),
        out_specs=(P(("row", "col"), None), P(("col", "row"), None)),
        check_vma=False,
    )
```

```python
import functools

import jax
import jax.numpy as jnp
from jax import lax
from jax.experimental import pallas as pl
from jax.experimental.pallas import tpu as pltpu
from jax.sharding import PartitionSpec as P


def silu_slope(mixed):
    sigma = jax.nn.sigmoid(mixed)
    return sigma * (1.0 + mixed * (1.0 - sigma))


def dense_layer(summed, grad_rows, weight):
    aggregated = summed.astype(jnp.bfloat16)
    mixed = jnp.dot(aggregated, weight, preferred_element_type=jnp.float32)
    activated = jax.nn.silu(mixed).astype(jnp.bfloat16)
    scaled = (grad_rows.astype(jnp.float32) * silu_slope(mixed)).astype(jnp.bfloat16)
    pulled = jnp.dot(scaled, weight.T, preferred_element_type=jnp.float32).astype(jnp.bfloat16)
    return (activated, pulled)


UNROLL = 4


def run_slots(count, product, place):
    def group(g, carry):
        base = g * UNROLL
        values = [product(base + j) for j in range(UNROLL)]
        for j, value in enumerate(values):
            place(base + j, value)
        return carry

    def single(k, carry):
        place(k, product(k))
        return carry

    lax.fori_loop(0, count // UNROLL, group, 0)
    lax.fori_loop((count // UNROLL) * UNROLL, count, single, 0)


def split_out(acc_ref, own_ref, send_refs, me):
    chunk = own_ref.shape[0]
    n = len(send_refs) + 1
    own_ref[...] = acc_ref[pl.ds(pl.multiple_of(me * chunk, 8), chunk), :]
    for shift in range(1, n):
        start = pl.multiple_of(((me + shift) % n) * chunk, 8)
        send_refs[shift - 1][...] = acc_ref[pl.ds(start, chunk), :].astype(send_refs[shift - 1].dtype)


def forward_kernel(chips, rows_ref, cols_ref, info_ref, a_ref, *rest):
    near_refs, far_refs = rest[:chips], rest[chips : 2 * chips]
    own_ref = rest[2 * chips]
    send_refs, f_ref, acc_ref = rest[2 * chips + 1 : -2], rest[-2], rest[-1]
    tile = a_ref.shape[1]
    piece = near_refs[0].shape[0]
    me = lax.axis_index("row")
    core, chip = me % 2, me // 2
    for shift in range(chips):
        owner = (chip - shift + chips) % chips
        near = pl.multiple_of((owner * 2 + core) * piece, 16)
        far = pl.multiple_of((owner * 2 + 1 - core) * piece, 16)
        f_ref[pl.ds(near, piece), :] = near_refs[shift][...]
        f_ref[pl.ds(far, piece), :] = far_refs[shift][...]
    acc_ref[...] = jnp.zeros_like(acc_ref)

    def product(k):
        f = f_ref[pl.ds(pl.multiple_of(cols_ref[k] * tile, tile), tile), :]
        return jnp.dot(a_ref[k], f, preferred_element_type=jnp.float32)

    def place(k, value):
        rows = pl.ds(pl.multiple_of(rows_ref[k] * tile, tile), tile)
        acc_ref[rows, :] += value

    run_slots(jnp.minimum(info_ref[0], a_ref.shape[0]), product, place)
    split_out(acc_ref, own_ref, send_refs, lax.axis_index("col"))


def backward_kernel(n, rows_ref, cols_ref, info_ref, a_ref, mine_ref, *rest):
    got_refs = rest[: n - 1]
    near_ref, far_ref, block_ref, acc_ref = rest[n - 1:]
    tile = a_ref.shape[1]
    chunk = mine_ref.shape[0]
    me = lax.axis_index("col")
    block_ref[pl.ds(pl.multiple_of(me * chunk, 16), chunk), :] = mine_ref[...]
    for shift in range(1, n):
        start = pl.multiple_of(((me - shift + n) % n) * chunk, 16)
        block_ref[pl.ds(start, chunk), :] = got_refs[shift - 1][...]
    acc_ref[...] = jnp.zeros_like(acc_ref)

    def product(k):
        p = block_ref[pl.ds(pl.multiple_of(rows_ref[k] * tile, tile), tile), :]
        return lax.dot_general(
            a_ref[k], p, (((0,), (0,)), ((), ())), preferred_element_type=jnp.float32
        )

    def place(k, value):
        cols = pl.ds(pl.multiple_of(cols_ref[k] * tile, tile), tile)
        acc_ref[cols, :] += value

    run_slots(jnp.minimum(info_ref[0], a_ref.shape[0]), product, place)
    chips = near_ref.shape[0]
    piece = near_ref.shape[1]
    me_row = lax.axis_index("row")
    core, chip = me_row % 2, me_row // 2
    for shift in range(chips):
        owner = (chip + shift) % chips
        near_ref[shift] = acc_ref[pl.ds(pl.multiple_of((owner * 2 + core) * piece, 8), piece), :]
        far_ref[shift] = acc_ref[pl.ds(pl.multiple_of((owner * 2 + 1 - core) * piece, 8), piece), :]


SMEM = pl.BlockSpec(memory_space=pltpu.SMEM)
VMEM = pl.BlockSpec(memory_space=pltpu.VMEM)


def tile_products(rows, cols, info, blocks, near, far, parts):
    out_rows = parts[0] * parts[1]
    chunk = parts[1]
    width = near[0].shape[1]
    return pl.pallas_call(
        functools.partial(forward_kernel, len(near)),
        out_shape=(jax.ShapeDtypeStruct((chunk, width), jnp.float32),)
        + (jax.ShapeDtypeStruct((chunk, width), jnp.bfloat16),) * (parts[0] - 1),
        in_specs=[SMEM, SMEM, SMEM, VMEM] + [VMEM] * (2 * len(near)),
        out_specs=(VMEM,) * parts[0],
        scratch_shapes=[
            pltpu.VMEM((2 * len(near) * near[0].shape[0], width), jnp.bfloat16),
            pltpu.VMEM((out_rows, width), jnp.float32),
        ],
    )(rows, cols, info, blocks, *near, *far)


def tile_products_t(rows, cols, info, blocks, mine, got, n_out, out_rows):
    chunk = out_rows // n_out
    width = mine.shape[1]
    stack = jax.ShapeDtypeStruct((n_out // 2, chunk, width), jnp.float32)
    return pl.pallas_call(
        functools.partial(backward_kernel, len(got) + 1),
        out_shape=(stack, stack),
        in_specs=[SMEM, SMEM, SMEM, VMEM, VMEM] + [VMEM] * len(got),
        out_specs=(VMEM, VMEM),
        scratch_shapes=[
            pltpu.VMEM(((len(got) + 1) * mine.shape[0], width), jnp.bfloat16),
            pltpu.VMEM((out_rows, width), jnp.float32),
        ],
    )(rows, cols, info, blocks, mine, *got)


def shifts(axis):
    n = lax.axis_size(axis)
    return [[(i, (i + shift) % n) for i in range(n)] for shift in range(1, n)]


def chip_shifts(n):
    chips = n // 2
    return [[(i, ((i // 2 + shift) % chips) * 2 + i % 2) for i in range(n)] for shift in range(1, chips)]


def partner(n):
    return [(i, i ^ 1) for i in range(n)]


def on_device(features, edge_tiles, tile_rows, tile_cols, tile_count, weight, cotangent):
    blocks = edge_tiles[0, 0]
    row_slots = tile_rows[0, 0]
    col_slots = tile_cols[0, 0]
    n_row = lax.axis_size("row")
    n_col = lax.axis_size("col")
    own_rows = features.shape[0]

    near = [features] + [lax.ppermute(features, "row", perm) for perm in chip_shifts(n_row)]
    far = [lax.ppermute(piece, "row", partner(n_row)) for piece in near]
    info = tile_count.reshape(1)
    own, *send = tile_products(row_slots, col_slots, info, blocks, near, far, (n_col, own_rows))
    total = own
    for shift, perm in enumerate(shifts("col")):
        total = total + lax.ppermute(send[shift], "col", perm).astype(jnp.float32)
    activated, pulled_own = dense_layer(total, cotangent, weight)
    got = [lax.ppermute(pulled_own, "col", perm) for perm in shifts("col")]
    near_g, far_g = tile_products_t(
        row_slots, col_slots, info, blocks, pulled_own, got, n_row, n_row * own_rows
    )
    chip_sums = near_g + lax.ppermute(far_g, "row", partner(n_row))
    total_g = chip_sums[0]
    for shift, perm in enumerate(chip_shifts(n_row)):
        piece = chip_sums[shift + 1].astype(jnp.bfloat16)
        total_g = total_g + lax.ppermute(piece, "row", perm).astype(jnp.float32)
    return (activated, total_g.astype(jnp.bfloat16))


def solution(mesh):
    return jax.shard_map(
        on_device,
        mesh=mesh,
        in_specs=(
            P(("col", "row"), None),
            P("row", "col", None, None, None),
            P("row", "col", None),
            P("row", "col", None),
            P("row", "col"),
            P(),
            P(("row", "col"), None),
        ),
        out_specs=(P(("row", "col"), None), P(("col", "row"), None)),
        check_vma=False,
    )
```

```python
import functools

import jax
import jax.numpy as jnp
from jax import lax
from jax.experimental import pallas as pl
from jax.experimental.pallas import tpu as pltpu
from jax.sharding import PartitionSpec as P

SMEM = pl.BlockSpec(memory_space=pltpu.SMEM)
VMEM = pl.BlockSpec(memory_space=pltpu.VMEM)


UNROLL = 4


def run_slots(count, product, place):
    def group(g, carry):
        base = g * UNROLL
        values = [product(base + j) for j in range(UNROLL)]
        for j, value in enumerate(values):
            place(base + j, value)
        return carry

    def single(k, carry):
        place(k, product(k))
        return carry

    lax.fori_loop(0, count // UNROLL, group, 0)
    lax.fori_loop((count // UNROLL) * UNROLL, count, single, 0)


def split_out(acc_ref, own_ref, send_refs, me):
    chunk = own_ref.shape[0]
    n = len(send_refs) + 1
    own_ref[...] = acc_ref[pl.ds(pl.multiple_of(me * chunk, 8), chunk), :]
    for shift in range(1, n):
        start = pl.multiple_of(((me + shift) % n) * chunk, 8)
        send_refs[shift - 1][...] = acc_ref[pl.ds(start, chunk), :].astype(send_refs[shift - 1].dtype)


def forward_kernel(rows_ref, cols_ref, info_ref, a_ref, near_ref, far_ref, own_ref, *rest):
    send_refs, f_ref, acc_ref = rest[:-2], rest[-2], rest[-1]
    tile = a_ref.shape[1]
    chips, piece = near_ref.shape[0], near_ref.shape[1]
    me = lax.axis_index("row")
    core, chip = me % 2, me // 2
    for shift in range(chips):
        owner = (chip - shift + chips) % chips
        near = pl.multiple_of((owner * 2 + core) * piece, 16)
        far = pl.multiple_of((owner * 2 + 1 - core) * piece, 16)
        f_ref[pl.ds(near, piece), :] = near_ref[shift]
        f_ref[pl.ds(far, piece), :] = far_ref[shift]
    acc_ref[...] = jnp.zeros_like(acc_ref)

    def product(k):
        f = f_ref[pl.ds(pl.multiple_of(cols_ref[k] * tile, tile), tile), :]
        return jnp.dot(a_ref[k], f, preferred_element_type=jnp.float32)

    def place(k, value):
        rows = pl.ds(pl.multiple_of(rows_ref[k] * tile, tile), tile)
        acc_ref[rows, :] += value

    run_slots(jnp.minimum(info_ref[0], a_ref.shape[0]), product, place)
    split_out(acc_ref, own_ref, send_refs, lax.axis_index("col"))


def backward_kernel(n, rows_ref, cols_ref, info_ref, a_ref, weight_ref, *rest):
    agg_refs, cot_refs = rest[:n], rest[n : 2 * n]
    act_ref, near_ref, far_ref, agg_block, cot_block, act_block, block_ref, acc_ref = rest[2 * n :]
    tile = a_ref.shape[1]
    chunk = agg_refs[0].shape[0]
    me = lax.axis_index("col")
    for shift in range(n):
        start = pl.multiple_of(((me - shift + n) % n) * chunk, 16)
        agg_block[pl.ds(start, chunk), :] = agg_refs[shift][...]
        cot_block[pl.ds(start, chunk), :] = cot_refs[shift][...]
    weight = weight_ref[...]
    mixed = jnp.dot(agg_block[...], weight, preferred_element_type=jnp.float32)
    sigma = jax.nn.sigmoid(mixed)
    act_block[...] = mixed * sigma
    act_ref[...] = act_block[pl.ds(pl.multiple_of(me * chunk, 8), chunk), :].astype(act_ref.dtype)
    slope = sigma * (1.0 + mixed * (1.0 - sigma))
    scaled = (cot_block[...].astype(jnp.float32) * slope).astype(jnp.bfloat16)
    block_ref[...] = lax.dot_general(
        scaled, weight, (((1,), (1,)), ((), ())), preferred_element_type=jnp.float32
    ).astype(block_ref.dtype)
    acc_ref[...] = jnp.zeros_like(acc_ref)

    def product(k):
        p = block_ref[pl.ds(pl.multiple_of(rows_ref[k] * tile, tile), tile), :]
        return lax.dot_general(
            a_ref[k], p, (((0,), (0,)), ((), ())), preferred_element_type=jnp.float32
        )

    def place(k, value):
        cols = pl.ds(pl.multiple_of(cols_ref[k] * tile, tile), tile)
        acc_ref[cols, :] += value

    run_slots(jnp.minimum(info_ref[0], a_ref.shape[0]), product, place)
    chips = near_ref.shape[0]
    piece = near_ref.shape[1]
    me_row = lax.axis_index("row")
    core, chip = me_row % 2, me_row // 2
    for shift in range(chips):
        owner = (chip + shift) % chips
        near_ref[shift] = acc_ref[pl.ds(pl.multiple_of((owner * 2 + core) * piece, 8), piece), :]
        far_ref[shift] = acc_ref[pl.ds(pl.multiple_of((owner * 2 + 1 - core) * piece, 8), piece), :]


def tile_products(rows, cols, info, blocks, near, far, parts):
    out_rows = parts[0] * parts[1]
    chunk = parts[1]
    width = near.shape[2]
    return pl.pallas_call(
        forward_kernel,
        out_shape=(jax.ShapeDtypeStruct((chunk, width), jnp.float32),)
        + (jax.ShapeDtypeStruct((chunk, width), jnp.bfloat16),) * (parts[0] - 1),
        in_specs=[SMEM, SMEM, SMEM, VMEM, VMEM, VMEM],
        out_specs=(VMEM,) * parts[0],
        scratch_shapes=[
            pltpu.VMEM((2 * near.shape[0] * near.shape[1], width), jnp.bfloat16),
            pltpu.VMEM((out_rows, width), jnp.float32),
        ],
    )(rows, cols, info, blocks, near, far)


def tile_products_t(rows, cols, info, blocks, weight, aggs, cots, n_out, out_rows):
    chunk = out_rows // n_out
    width = aggs[0].shape[1]
    block_rows = len(aggs) * aggs[0].shape[0]
    stack = jax.ShapeDtypeStruct((n_out // 2, chunk, width), jnp.float32)
    return pl.pallas_call(
        functools.partial(backward_kernel, len(aggs)),
        out_shape=(jax.ShapeDtypeStruct(aggs[0].shape, jnp.bfloat16), stack, stack),
        in_specs=[SMEM, SMEM, SMEM, VMEM, VMEM] + [VMEM] * (2 * len(aggs)),
        out_specs=(VMEM, VMEM, VMEM),
        scratch_shapes=[
            pltpu.VMEM((block_rows, width), jnp.bfloat16),
            pltpu.VMEM((block_rows, width), jnp.bfloat16),
            pltpu.VMEM((block_rows, width), jnp.float32),
            pltpu.VMEM((block_rows, width), jnp.bfloat16),
            pltpu.VMEM((out_rows, width), jnp.float32),
        ],
    )(rows, cols, info, blocks, weight, *aggs, *cots)


def shifts(axis):
    n = lax.axis_size(axis)
    return [[(i, (i + shift) % n) for i in range(n)] for shift in range(1, n)]


def chip_shifts(n):
    chips = n // 2
    return [[(i, ((i // 2 + shift) % chips) * 2 + i % 2) for i in range(n)] for shift in range(1, chips)]


def partner(n):
    return [(i, i ^ 1) for i in range(n)]


def on_device(features, edge_tiles, tile_rows, tile_cols, tile_count, weight, cotangent):
    blocks = edge_tiles[0, 0]
    row_slots = tile_rows[0, 0]
    col_slots = tile_cols[0, 0]
    n_row = lax.axis_size("row")
    n_col = lax.axis_size("col")
    own_rows = features.shape[0]

    cots = [cotangent] + [lax.ppermute(cotangent, "col", perm) for perm in shifts("col")]
    pieces = [features] + [lax.ppermute(features, "row", perm) for perm in chip_shifts(n_row)]
    pieces, cots = lax.optimization_barrier((pieces, cots))
    near = jnp.stack(pieces)
    far = lax.ppermute(near, "row", partner(n_row))
    info = tile_count.reshape(1)
    own, *send = tile_products(row_slots, col_slots, info, blocks, near, far, (n_col, own_rows))
    total = own
    for shift, perm in enumerate(shifts("col")):
        total = total + lax.ppermute(send[shift], "col", perm).astype(jnp.float32)
    aggregated = total.astype(jnp.bfloat16)
    aggs = [aggregated] + [lax.ppermute(aggregated, "col", perm) for perm in shifts("col")]
    activated, near_g, far_g = tile_products_t(
        row_slots, col_slots, info, blocks, weight, aggs, cots, n_row, n_row * own_rows
    )
    chip_sums = near_g + lax.ppermute(far_g, "row", partner(n_row))
    total_g = chip_sums[0]
    for shift, perm in enumerate(chip_shifts(n_row)):
        piece = chip_sums[shift + 1].astype(jnp.bfloat16)
        total_g = total_g + lax.ppermute(piece, "row", perm).astype(jnp.float32)
    return (activated, total_g.astype(jnp.bfloat16))


def solution(mesh):
    return jax.shard_map(
        on_device,
        mesh=mesh,
        in_specs=(
            P(("col", "row"), None),
            P("row", "col", None, None, None),
            P("row", "col", None),
            P("row", "col", None),
            P("row", "col"),
            P(),
            P(("row", "col"), None),
        ),
        out_specs=(P(("row", "col"), None), P(("col", "row"), None)),
        check_vma=False,
    )
```

```python
import functools

import jax
import jax.numpy as jnp
from jax import lax
from jax.experimental import pallas as pl
from jax.experimental.pallas import tpu as pltpu
from jax.sharding import PartitionSpec as P


def dense_kernel(n, own_ref, *rest):
    got_refs = rest[: n - 1]
    grad_ref, weight_ref, act_ref, pulled_ref = rest[n - 1:]
    total = own_ref[...]
    for got in got_refs:
        total = total + got[...].astype(jnp.float32)
    weight = weight_ref[...]
    mixed = jnp.dot(total.astype(jnp.bfloat16), weight, preferred_element_type=jnp.float32)
    sigma = jax.nn.sigmoid(mixed)
    act_ref[...] = (mixed * sigma).astype(act_ref.dtype)
    slope = sigma * (1.0 + mixed * (1.0 - sigma))
    scaled = (grad_ref[...].astype(jnp.float32) * slope).astype(jnp.bfloat16)
    pulled_ref[...] = lax.dot_general(
        scaled, weight, (((1,), (1,)), ((), ())), preferred_element_type=jnp.float32
    ).astype(pulled_ref.dtype)


def dense_layer_kernel(own, got, grad_rows, weight):
    shape = jax.ShapeDtypeStruct(own.shape, jnp.bfloat16)
    return pl.pallas_call(
        functools.partial(dense_kernel, len(got) + 1),
        out_shape=(shape, shape),
        in_specs=[VMEM] * (len(got) + 3),
        out_specs=(VMEM, VMEM),
    )(own, *got, grad_rows, weight)


UNROLL = 4


def run_slots(count, product, place):
    def group(g, carry):
        base = g * UNROLL
        values = [product(base + j) for j in range(UNROLL)]
        for j, value in enumerate(values):
            place(base + j, value)
        return carry

    def single(k, carry):
        place(k, product(k))
        return carry

    lax.fori_loop(0, count // UNROLL, group, 0)
    lax.fori_loop((count // UNROLL) * UNROLL, count, single, 0)


def split_out(acc_ref, own_ref, send_refs, me):
    chunk = own_ref.shape[0]
    n = len(send_refs) + 1
    own_ref[...] = acc_ref[pl.ds(pl.multiple_of(me * chunk, 8), chunk), :]
    for shift in range(1, n):
        start = pl.multiple_of(((me + shift) % n) * chunk, 8)
        send_refs[shift - 1][...] = acc_ref[pl.ds(start, chunk), :].astype(send_refs[shift - 1].dtype)


def forward_kernel(rows_ref, cols_ref, info_ref, a_ref, near_ref, far_ref, own_ref, *rest):
    send_refs, f_ref, acc_ref = rest[:-2], rest[-2], rest[-1]
    tile = a_ref.shape[1]
    chips, piece = near_ref.shape[0], near_ref.shape[1]
    me = lax.axis_index("row")
    core, chip = me % 2, me // 2
    for shift in range(chips):
        owner = (chip - shift + chips) % chips
        near = pl.multiple_of((owner * 2 + core) * piece, 16)
        far = pl.multiple_of((owner * 2 + 1 - core) * piece, 16)
        f_ref[pl.ds(near, piece), :] = near_ref[shift]
        f_ref[pl.ds(far, piece), :] = far_ref[shift]
    acc_ref[...] = jnp.zeros_like(acc_ref)

    def product(k):
        f = f_ref[pl.ds(pl.multiple_of(cols_ref[k] * tile, tile), tile), :]
        return jnp.dot(a_ref[k], f, preferred_element_type=jnp.float32)

    def place(k, value):
        rows = pl.ds(pl.multiple_of(rows_ref[k] * tile, tile), tile)
        acc_ref[rows, :] += value

    run_slots(jnp.minimum(info_ref[0], a_ref.shape[0]), product, place)
    split_out(acc_ref, own_ref, send_refs, lax.axis_index("col"))


def backward_kernel(n, rows_ref, cols_ref, info_ref, a_ref, mine_ref, *rest):
    got_refs = rest[: n - 1]
    near_ref, far_ref, block_ref, acc_ref = rest[n - 1:]
    tile = a_ref.shape[1]
    chunk = mine_ref.shape[0]
    me = lax.axis_index("col")
    block_ref[pl.ds(pl.multiple_of(me * chunk, 16), chunk), :] = mine_ref[...]
    for shift in range(1, n):
        start = pl.multiple_of(((me - shift + n) % n) * chunk, 16)
        block_ref[pl.ds(start, chunk), :] = got_refs[shift - 1][...]
    acc_ref[...] = jnp.zeros_like(acc_ref)

    def product(k):
        p = block_ref[pl.ds(pl.multiple_of(rows_ref[k] * tile, tile), tile), :]
        return lax.dot_general(
            a_ref[k], p, (((0,), (0,)), ((), ())), preferred_element_type=jnp.float32
        )

    def place(k, value):
        cols = pl.ds(pl.multiple_of(cols_ref[k] * tile, tile), tile)
        acc_ref[cols, :] += value

    run_slots(jnp.minimum(info_ref[0], a_ref.shape[0]), product, place)
    chips = near_ref.shape[0]
    piece = near_ref.shape[1]
    me_row = lax.axis_index("row")
    core, chip = me_row % 2, me_row // 2
    for shift in range(chips):
        owner = (chip + shift) % chips
        near_ref[shift] = acc_ref[pl.ds(pl.multiple_of((owner * 2 + core) * piece, 8), piece), :]
        far_ref[shift] = acc_ref[pl.ds(pl.multiple_of((owner * 2 + 1 - core) * piece, 8), piece), :]


SMEM = pl.BlockSpec(memory_space=pltpu.SMEM)
VMEM = pl.BlockSpec(memory_space=pltpu.VMEM)


def tile_products(rows, cols, info, blocks, near, far, parts):
    out_rows = parts[0] * parts[1]
    chunk = parts[1]
    width = near.shape[2]
    return pl.pallas_call(
        forward_kernel,
        out_shape=(jax.ShapeDtypeStruct((chunk, width), jnp.float32),)
        + (jax.ShapeDtypeStruct((chunk, width), jnp.bfloat16),) * (parts[0] - 1),
        in_specs=[SMEM, SMEM, SMEM, VMEM, VMEM, VMEM],
        out_specs=(VMEM,) * parts[0],
        scratch_shapes=[
            pltpu.VMEM((2 * near.shape[0] * near.shape[1], width), jnp.bfloat16),
            pltpu.VMEM((out_rows, width), jnp.float32),
        ],
    )(rows, cols, info, blocks, near, far)


def tile_products_t(rows, cols, info, blocks, mine, got, n_out, out_rows):
    chunk = out_rows // n_out
    width = mine.shape[1]
    stack = jax.ShapeDtypeStruct((n_out // 2, chunk, width), jnp.float32)
    return pl.pallas_call(
        functools.partial(backward_kernel, len(got) + 1),
        out_shape=(stack, stack),
        in_specs=[SMEM, SMEM, SMEM, VMEM, VMEM] + [VMEM] * len(got),
        out_specs=(VMEM, VMEM),
        scratch_shapes=[
            pltpu.VMEM(((len(got) + 1) * mine.shape[0], width), jnp.bfloat16),
            pltpu.VMEM((out_rows, width), jnp.float32),
        ],
    )(rows, cols, info, blocks, mine, *got)


def shifts(axis):
    n = lax.axis_size(axis)
    return [[(i, (i + shift) % n) for i in range(n)] for shift in range(1, n)]


def chip_shifts(n):
    chips = n // 2
    return [[(i, ((i // 2 + shift) % chips) * 2 + i % 2) for i in range(n)] for shift in range(1, chips)]


def partner(n):
    return [(i, i ^ 1) for i in range(n)]


def on_device(features, edge_tiles, tile_rows, tile_cols, tile_count, weight, cotangent):
    blocks = edge_tiles[0, 0]
    row_slots = tile_rows[0, 0]
    col_slots = tile_cols[0, 0]
    n_row = lax.axis_size("row")
    n_col = lax.axis_size("col")
    own_rows = features.shape[0]

    near = jnp.stack([features] + [lax.ppermute(features, "row", perm) for perm in chip_shifts(n_row)])
    far = lax.ppermute(near, "row", partner(n_row))
    info = tile_count.reshape(1)
    own, *send = tile_products(row_slots, col_slots, info, blocks, near, far, (n_col, own_rows))
    got_f = [lax.ppermute(send[shift], "col", perm) for shift, perm in enumerate(shifts("col"))]
    activated, pulled_own = dense_layer_kernel(own, got_f, cotangent, weight)
    got = [lax.ppermute(pulled_own, "col", perm) for perm in shifts("col")]
    near_g, far_g = tile_products_t(
        row_slots, col_slots, info, blocks, pulled_own, got, n_row, n_row * own_rows
    )
    chip_sums = near_g + lax.ppermute(far_g, "row", partner(n_row))
    total_g = chip_sums[0]
    for shift, perm in enumerate(chip_shifts(n_row)):
        piece = chip_sums[shift + 1].astype(jnp.bfloat16)
        total_g = total_g + lax.ppermute(piece, "row", perm).astype(jnp.float32)
    return (activated, total_g.astype(jnp.bfloat16))


def solution(mesh):
    return jax.shard_map(
        on_device,
        mesh=mesh,
        in_specs=(
            P(("col", "row"), None),
            P("row", "col", None, None, None),
            P("row", "col", None),
            P("row", "col", None),
            P("row", "col"),
            P(),
            P(("row", "col"), None),
        ),
        out_specs=(P(("row", "col"), None), P(("col", "row"), None)),
        check_vma=False,
    )
```

```python
import functools

import jax
import jax.numpy as jnp
from jax import lax
from jax.experimental import pallas as pl
from jax.experimental.pallas import tpu as pltpu
from jax.sharding import PartitionSpec as P


def silu_slope(mixed):
    sigma = jax.nn.sigmoid(mixed)
    return sigma * (1.0 + mixed * (1.0 - sigma))


def dense_layer(summed, grad_rows, weight):
    aggregated = summed.astype(jnp.bfloat16)
    mixed = jnp.dot(aggregated, weight, preferred_element_type=jnp.float32)
    activated = jax.nn.silu(mixed).astype(jnp.bfloat16)
    scaled = (grad_rows.astype(jnp.float32) * silu_slope(mixed)).astype(jnp.bfloat16)
    pulled = jnp.dot(scaled, weight.T, preferred_element_type=jnp.float32).astype(jnp.bfloat16)
    return (activated, pulled)


UNROLL = 4


def run_slots(count, product, place):
    def group(g, carry):
        base = g * UNROLL
        values = [product(base + j) for j in range(UNROLL)]
        for j, value in enumerate(values):
            place(base + j, value)
        return carry

    def single(k, carry):
        place(k, product(k))
        return carry

    lax.fori_loop(0, count // UNROLL, group, 0)
    lax.fori_loop((count // UNROLL) * UNROLL, count, single, 0)


def split_out(acc_ref, own_ref, send_refs, me):
    chunk = own_ref.shape[0]
    n = len(send_refs) + 1
    own_ref[...] = acc_ref[pl.ds(pl.multiple_of(me * chunk, 8), chunk), :]
    for shift in range(1, n):
        start = pl.multiple_of(((me + shift) % n) * chunk, 8)
        send_refs[shift - 1][...] = acc_ref[pl.ds(start, chunk), :].astype(send_refs[shift - 1].dtype)


def forward_kernel(rows_ref, cols_ref, info_ref, a_ref, near_ref, far_ref, own_ref, *rest):
    send_refs, f_ref, acc_ref = rest[:-2], rest[-2], rest[-1]
    tile = a_ref.shape[1]
    chips, piece = near_ref.shape[0], near_ref.shape[1]
    me = lax.axis_index("row")
    core, chip = me % 2, me // 2
    for shift in range(chips):
        owner = (chip - shift + chips) % chips
        near = pl.multiple_of((owner * 2 + core) * piece, 16)
        far = pl.multiple_of((owner * 2 + 1 - core) * piece, 16)
        f_ref[pl.ds(near, piece), :] = near_ref[shift]
        f_ref[pl.ds(far, piece), :] = far_ref[shift]
    acc_ref[...] = jnp.zeros_like(acc_ref)

    def product(k):
        f = f_ref[pl.ds(pl.multiple_of(cols_ref[k] * tile, tile), tile), :]
        return jnp.dot(a_ref[k], f, preferred_element_type=jnp.float32)

    def place(k, value):
        rows = pl.ds(pl.multiple_of(rows_ref[k] * tile, tile), tile)
        acc_ref[rows, :] += value

    run_slots(jnp.minimum(info_ref[0], a_ref.shape[0]), product, place)
    split_out(acc_ref, own_ref, send_refs, lax.axis_index("col"))


def backward_kernel(n, rows_ref, cols_ref, info_ref, a_ref, mine_ref, *rest):
    got_refs = rest[: n - 1]
    near_ref, far_ref, block_ref, acc_ref = rest[n - 1:]
    tile = a_ref.shape[1]
    chunk = mine_ref.shape[0]
    me = lax.axis_index("col")
    block_ref[pl.ds(pl.multiple_of(me * chunk, 16), chunk), :] = mine_ref[...]
    for shift in range(1, n):
        start = pl.multiple_of(((me - shift + n) % n) * chunk, 16)
        block_ref[pl.ds(start, chunk), :] = got_refs[shift - 1][...]
    acc_ref[...] = jnp.zeros_like(acc_ref)

    def product(k):
        p = block_ref[pl.ds(pl.multiple_of(rows_ref[k] * tile, tile), tile), :]
        return lax.dot_general(
            a_ref[k], p, (((0,), (0,)), ((), ())), preferred_element_type=jnp.float32
        )

    def place(k, value):
        cols = pl.ds(pl.multiple_of(cols_ref[k] * tile, tile), tile)
        acc_ref[cols, :] += value

    run_slots(jnp.minimum(info_ref[0], a_ref.shape[0]), product, place)
    chips = near_ref.shape[0]
    piece = near_ref.shape[1]
    me_row = lax.axis_index("row")
    core, chip = me_row % 2, me_row // 2
    for shift in range(chips):
        owner = (chip + shift) % chips
        near_ref[shift] = acc_ref[pl.ds(pl.multiple_of((owner * 2 + core) * piece, 8), piece), :]
        far_ref[shift] = acc_ref[pl.ds(pl.multiple_of((owner * 2 + 1 - core) * piece, 8), piece), :].astype(
            far_ref.dtype
        )


SMEM = pl.BlockSpec(memory_space=pltpu.SMEM)
VMEM = pl.BlockSpec(memory_space=pltpu.VMEM)


def tile_products(rows, cols, info, blocks, near, far, parts):
    out_rows = parts[0] * parts[1]
    chunk = parts[1]
    width = near.shape[2]
    return pl.pallas_call(
        forward_kernel,
        out_shape=(jax.ShapeDtypeStruct((chunk, width), jnp.float32),)
        + (jax.ShapeDtypeStruct((chunk, width), jnp.bfloat16),) * (parts[0] - 1),
        in_specs=[SMEM, SMEM, SMEM, VMEM, VMEM, VMEM],
        out_specs=(VMEM,) * parts[0],
        scratch_shapes=[
            pltpu.VMEM((2 * near.shape[0] * near.shape[1], width), jnp.bfloat16),
            pltpu.VMEM((out_rows, width), jnp.float32),
        ],
    )(rows, cols, info, blocks, near, far)


def tile_products_t(rows, cols, info, blocks, mine, got, n_out, out_rows):
    chunk = out_rows // n_out
    width = mine.shape[1]
    near = jax.ShapeDtypeStruct((n_out // 2, chunk, width), jnp.float32)
    far = jax.ShapeDtypeStruct((n_out // 2, chunk, width), jnp.bfloat16)
    return pl.pallas_call(
        functools.partial(backward_kernel, len(got) + 1),
        out_shape=(near, far),
        in_specs=[SMEM, SMEM, SMEM, VMEM, VMEM] + [VMEM] * len(got),
        out_specs=(VMEM, VMEM),
        scratch_shapes=[
            pltpu.VMEM(((len(got) + 1) * mine.shape[0], width), jnp.bfloat16),
            pltpu.VMEM((out_rows, width), jnp.float32),
        ],
    )(rows, cols, info, blocks, mine, *got)


def shifts(axis):
    n = lax.axis_size(axis)
    return [[(i, (i + shift) % n) for i in range(n)] for shift in range(1, n)]


def chip_shifts(n):
    chips = n // 2
    return [[(i, ((i // 2 + shift) % chips) * 2 + i % 2) for i in range(n)] for shift in range(1, chips)]


def partner(n):
    return [(i, i ^ 1) for i in range(n)]


def on_device(features, edge_tiles, tile_rows, tile_cols, tile_count, weight, cotangent):
    blocks = edge_tiles[0, 0]
    row_slots = tile_rows[0, 0]
    col_slots = tile_cols[0, 0]
    n_row = lax.axis_size("row")
    n_col = lax.axis_size("col")
    own_rows = features.shape[0]

    near = jnp.stack([features] + [lax.ppermute(features, "row", perm) for perm in chip_shifts(n_row)])
    far = lax.ppermute(near, "row", partner(n_row))
    info = tile_count.reshape(1)
    own, *send = tile_products(row_slots, col_slots, info, blocks, near, far, (n_col, own_rows))
    total = own
    for shift, perm in enumerate(shifts("col")):
        total = total + lax.ppermute(send[shift], "col", perm).astype(jnp.float32)
    activated, pulled_own = dense_layer(total, cotangent, weight)
    got = [lax.ppermute(pulled_own, "col", perm) for perm in shifts("col")]
    near_g, far_g = tile_products_t(
        row_slots, col_slots, info, blocks, pulled_own, got, n_row, n_row * own_rows
    )
    chip_sums = near_g + lax.ppermute(far_g, "row", partner(n_row)).astype(jnp.float32)
    total_g = chip_sums[0]
    for shift, perm in enumerate(chip_shifts(n_row)):
        piece = chip_sums[shift + 1].astype(jnp.bfloat16)
        total_g = total_g + lax.ppermute(piece, "row", perm).astype(jnp.float32)
    return (activated, total_g.astype(jnp.bfloat16))


def solution(mesh):
    return jax.shard_map(
        on_device,
        mesh=mesh,
        in_specs=(
            P(("col", "row"), None),
            P("row", "col", None, None, None),
            P("row", "col", None),
            P("row", "col", None),
            P("row", "col"),
            P(),
            P(("row", "col"), None),
        ),
        out_specs=(P(("row", "col"), None), P(("col", "row"), None)),
        check_vma=False,
    )
```

```python
import functools

import jax
import jax.numpy as jnp
from jax import lax
from jax.experimental import pallas as pl
from jax.experimental.pallas import tpu as pltpu
from jax.sharding import PartitionSpec as P


def silu_slope(mixed):
    sigma = jax.nn.sigmoid(mixed)
    return sigma * (1.0 + mixed * (1.0 - sigma))


def dense_layer(summed, grad_rows, weight):
    aggregated = summed.astype(jnp.bfloat16)
    mixed = jnp.dot(aggregated, weight, preferred_element_type=jnp.float32)
    activated = jax.nn.silu(mixed).astype(jnp.bfloat16)
    scaled = (grad_rows.astype(jnp.float32) * silu_slope(mixed)).astype(jnp.bfloat16)
    pulled = jnp.dot(scaled, weight.T, preferred_element_type=jnp.float32).astype(jnp.bfloat16)
    return (activated, pulled)


UNROLL = 4


def peer(i, step, n):
    return i ^ step if n & (n - 1) == 0 else (i + step) % n


def source(i, step, n):
    return i ^ step if n & (n - 1) == 0 else (i - step + n) % n


def run_slots(count, product, place):
    def group(g, carry):
        base = g * UNROLL
        values = [product(base + j) for j in range(UNROLL)]
        for j, value in enumerate(values):
            place(base + j, value)
        return carry

    def single(k, carry):
        place(k, product(k))
        return carry

    lax.fori_loop(0, count // UNROLL, group, 0)
    lax.fori_loop((count // UNROLL) * UNROLL, count, single, 0)


def split_out(acc_ref, own_ref, send_refs, me):
    chunk = own_ref.shape[0]
    n = len(send_refs) + 1
    own_ref[...] = acc_ref[pl.ds(pl.multiple_of(me * chunk, 8), chunk), :]
    for shift in range(1, n):
        start = pl.multiple_of(peer(me, shift, n) * chunk, 8)
        send_refs[shift - 1][...] = acc_ref[pl.ds(start, chunk), :].astype(send_refs[shift - 1].dtype)


def forward_kernel(rows_ref, cols_ref, info_ref, a_ref, near_ref, far_ref, own_ref, *rest):
    send_refs, f_ref, acc_ref = rest[:-2], rest[-2], rest[-1]
    tile = a_ref.shape[1]
    chips, piece = near_ref.shape[0], near_ref.shape[1]
    me = lax.axis_index("row")
    core, chip = me % 2, me // 2
    for shift in range(chips):
        owner = source(chip, shift, chips)
        near = pl.multiple_of((owner * 2 + core) * piece, 16)
        far = pl.multiple_of((owner * 2 + 1 - core) * piece, 16)
        f_ref[pl.ds(near, piece), :] = near_ref[shift]
        f_ref[pl.ds(far, piece), :] = far_ref[shift]
    acc_ref[...] = jnp.zeros_like(acc_ref)

    def product(k):
        f = f_ref[pl.ds(pl.multiple_of(cols_ref[k] * tile, tile), tile), :]
        return jnp.dot(a_ref[k], f, preferred_element_type=jnp.float32)

    def place(k, value):
        rows = pl.ds(pl.multiple_of(rows_ref[k] * tile, tile), tile)
        acc_ref[rows, :] += value

    run_slots(jnp.minimum(info_ref[0], a_ref.shape[0]), product, place)
    split_out(acc_ref, own_ref, send_refs, lax.axis_index("col"))


def backward_kernel(n, rows_ref, cols_ref, info_ref, a_ref, mine_ref, *rest):
    got_refs = rest[: n - 1]
    near_ref, far_ref, block_ref, acc_ref = rest[n - 1:]
    tile = a_ref.shape[1]
    chunk = mine_ref.shape[0]
    me = lax.axis_index("col")
    block_ref[pl.ds(pl.multiple_of(me * chunk, 16), chunk), :] = mine_ref[...]
    for shift in range(1, n):
        start = pl.multiple_of(source(me, shift, n) * chunk, 16)
        block_ref[pl.ds(start, chunk), :] = got_refs[shift - 1][...]
    acc_ref[...] = jnp.zeros_like(acc_ref)

    def product(k):
        p = block_ref[pl.ds(pl.multiple_of(rows_ref[k] * tile, tile), tile), :]
        return lax.dot_general(
            a_ref[k], p, (((0,), (0,)), ((), ())), preferred_element_type=jnp.float32
        )

    def place(k, value):
        cols = pl.ds(pl.multiple_of(cols_ref[k] * tile, tile), tile)
        acc_ref[cols, :] += value

    run_slots(jnp.minimum(info_ref[0], a_ref.shape[0]), product, place)
    chips = near_ref.shape[0]
    piece = near_ref.shape[1]
    me_row = lax.axis_index("row")
    core, chip = me_row % 2, me_row // 2
    for shift in range(chips):
        owner = peer(chip, shift, chips)
        near_ref[shift] = acc_ref[pl.ds(pl.multiple_of((owner * 2 + core) * piece, 8), piece), :]
        far_ref[shift] = acc_ref[pl.ds(pl.multiple_of((owner * 2 + 1 - core) * piece, 8), piece), :].astype(
            far_ref.dtype
        )


SMEM = pl.BlockSpec(memory_space=pltpu.SMEM)
VMEM = pl.BlockSpec(memory_space=pltpu.VMEM)


def tile_products(rows, cols, info, blocks, near, far, parts):
    out_rows = parts[0] * parts[1]
    chunk = parts[1]
    width = near.shape[2]
    return pl.pallas_call(
        forward_kernel,
        out_shape=(jax.ShapeDtypeStruct((chunk, width), jnp.float32),)
        + (jax.ShapeDtypeStruct((chunk, width), jnp.bfloat16),) * (parts[0] - 1),
        in_specs=[SMEM, SMEM, SMEM, VMEM, VMEM, VMEM],
        out_specs=(VMEM,) * parts[0],
        scratch_shapes=[
            pltpu.VMEM((2 * near.shape[0] * near.shape[1], width), jnp.bfloat16),
            pltpu.VMEM((out_rows, width), jnp.float32),
        ],
    )(rows, cols, info, blocks, near, far)


def tile_products_t(rows, cols, info, blocks, mine, got, n_out, out_rows):
    chunk = out_rows // n_out
    width = mine.shape[1]
    near = jax.ShapeDtypeStruct((n_out // 2, chunk, width), jnp.float32)
    far = jax.ShapeDtypeStruct((n_out // 2, chunk, width), jnp.bfloat16)
    return pl.pallas_call(
        functools.partial(backward_kernel, len(got) + 1),
        out_shape=(near, far),
        in_specs=[SMEM, SMEM, SMEM, VMEM, VMEM] + [VMEM] * len(got),
        out_specs=(VMEM, VMEM),
        scratch_shapes=[
            pltpu.VMEM(((len(got) + 1) * mine.shape[0], width), jnp.bfloat16),
            pltpu.VMEM((out_rows, width), jnp.float32),
        ],
    )(rows, cols, info, blocks, mine, *got)


def shifts(axis):
    n = lax.axis_size(axis)
    return [[(i, peer(i, shift, n)) for i in range(n)] for shift in range(1, n)]


def chip_shifts(n):
    chips = n // 2
    return [[(i, peer(i // 2, shift, chips) * 2 + i % 2) for i in range(n)] for shift in range(1, chips)]


def partner(n):
    return [(i, i ^ 1) for i in range(n)]


def on_device(features, edge_tiles, tile_rows, tile_cols, tile_count, weight, cotangent):
    blocks = edge_tiles[0, 0]
    row_slots = tile_rows[0, 0]
    col_slots = tile_cols[0, 0]
    n_row = lax.axis_size("row")
    n_col = lax.axis_size("col")
    own_rows = features.shape[0]

    near = jnp.stack([features] + [lax.ppermute(features, "row", perm) for perm in chip_shifts(n_row)])
    far = lax.ppermute(near, "row", partner(n_row))
    info = tile_count.reshape(1)
    own, *send = tile_products(row_slots, col_slots, info, blocks, near, far, (n_col, own_rows))
    total = own
    for shift, perm in enumerate(shifts("col")):
        total = total + lax.ppermute(send[shift], "col", perm).astype(jnp.float32)
    activated, pulled_own = dense_layer(total, cotangent, weight)
    got = [lax.ppermute(pulled_own, "col", perm) for perm in shifts("col")]
    near_g, far_g = tile_products_t(
        row_slots, col_slots, info, blocks, pulled_own, got, n_row, n_row * own_rows
    )
    chip_sums = near_g + lax.ppermute(far_g, "row", partner(n_row)).astype(jnp.float32)
    total_g = chip_sums[0]
    for shift, perm in enumerate(chip_shifts(n_row)):
        piece = chip_sums[shift + 1].astype(jnp.bfloat16)
        total_g = total_g + lax.ppermute(piece, "row", perm).astype(jnp.float32)
    return (activated, total_g.astype(jnp.bfloat16))


def solution(mesh):
    return jax.shard_map(
        on_device,
        mesh=mesh,
        in_specs=(
            P(("col", "row"), None),
            P("row", "col", None, None, None),
            P("row", "col", None),
            P("row", "col", None),
            P("row", "col"),
            P(),
            P(("row", "col"), None),
        ),
        out_specs=(P(("row", "col"), None), P(("col", "row"), None)),
        check_vma=False,
    )
```

```python
import functools

import jax
import jax.numpy as jnp
from jax import lax
from jax.experimental import pallas as pl
from jax.experimental.pallas import tpu as pltpu
from jax.sharding import PartitionSpec as P


def silu_slope(mixed):
    sigma = jax.nn.sigmoid(mixed)
    return sigma * (1.0 + mixed * (1.0 - sigma))


def dense_layer(summed, grad_rows, weight):
    aggregated = summed.astype(jnp.bfloat16)
    mixed = jnp.dot(aggregated, weight, preferred_element_type=jnp.float32)
    activated = jax.nn.silu(mixed).astype(jnp.bfloat16)
    scaled = (grad_rows.astype(jnp.float32) * silu_slope(mixed)).astype(jnp.bfloat16)
    pulled = jnp.dot(scaled, weight.T, preferred_element_type=jnp.float32).astype(jnp.bfloat16)
    return (activated, pulled)


UNROLL = 4


def run_slots(count, product, place):
    def group(g, carry):
        base = g * UNROLL
        values = [product(base + j) for j in range(UNROLL)]
        for j, value in enumerate(values):
            place(base + j, value)
        return carry

    def single(k, carry):
        place(k, product(k))
        return carry

    lax.fori_loop(0, count // UNROLL, group, 0)
    lax.fori_loop((count // UNROLL) * UNROLL, count, single, 0)


def split_out(acc_ref, own_ref, send_refs, me):
    chunk = own_ref.shape[0]
    n = len(send_refs) + 1
    own_ref[...] = acc_ref[pl.ds(pl.multiple_of(me * chunk, 8), chunk), :]
    for shift in range(1, n):
        start = pl.multiple_of(((me + shift) % n) * chunk, 8)
        send_refs[shift - 1][...] = acc_ref[pl.ds(start, chunk), :].astype(send_refs[shift - 1].dtype)


def forward_kernel(rows_ref, cols_ref, info_ref, a_ref, near_ref, far_ref, own_ref, *rest):
    send_refs, f_ref, acc_ref = rest[:-2], rest[-2], rest[-1]
    tile = a_ref.shape[1]
    chips, piece = near_ref.shape[0], near_ref.shape[1]
    me = lax.axis_index("row")
    core, chip = me % 2, me // 2
    for shift in range(chips):
        owner = (chip - shift + chips) % chips
        near = pl.multiple_of((owner * 2 + core) * piece, 16)
        far = pl.multiple_of((owner * 2 + 1 - core) * piece, 16)
        f_ref[pl.ds(near, piece), :] = near_ref[shift]
        f_ref[pl.ds(far, piece), :] = far_ref[shift]
    acc_ref[...] = jnp.zeros_like(acc_ref)

    def product(k):
        f = f_ref[pl.ds(pl.multiple_of(cols_ref[k] * tile, tile), tile), :]
        return jnp.dot(a_ref[k], f, preferred_element_type=jnp.float32)

    def place(k, value):
        rows = pl.ds(pl.multiple_of(rows_ref[k] * tile, tile), tile)
        acc_ref[rows, :] += value

    run_slots(jnp.minimum(info_ref[0], a_ref.shape[0]), product, place)
    me = lax.axis_index("col")
    chunk = own_ref.shape[0]
    n = send_refs[0].shape[0]
    own_ref[...] = acc_ref[pl.ds(pl.multiple_of(me * chunk, 8), chunk), :]
    for dest in range(n):
        send_refs[0][dest] = acc_ref[pl.ds(dest * chunk, chunk), :].astype(send_refs[0].dtype)
    send_refs[0][me] = jnp.zeros(send_refs[0].shape[1:], send_refs[0].dtype)


def backward_kernel(n, rows_ref, cols_ref, info_ref, a_ref, mine_ref, *rest):
    got_refs = rest[: n - 1]
    near_ref, far_ref, block_ref, acc_ref = rest[n - 1:]
    tile = a_ref.shape[1]
    chunk = mine_ref.shape[0]
    me = lax.axis_index("col")
    block_ref[pl.ds(pl.multiple_of(me * chunk, 16), chunk), :] = mine_ref[...]
    for shift in range(1, n):
        start = pl.multiple_of(((me - shift + n) % n) * chunk, 16)
        block_ref[pl.ds(start, chunk), :] = got_refs[shift - 1][...]
    acc_ref[...] = jnp.zeros_like(acc_ref)

    def product(k):
        p = block_ref[pl.ds(pl.multiple_of(rows_ref[k] * tile, tile), tile), :]
        return lax.dot_general(
            a_ref[k], p, (((0,), (0,)), ((), ())), preferred_element_type=jnp.float32
        )

    def place(k, value):
        cols = pl.ds(pl.multiple_of(cols_ref[k] * tile, tile), tile)
        acc_ref[cols, :] += value

    run_slots(jnp.minimum(info_ref[0], a_ref.shape[0]), product, place)
    chips = near_ref.shape[0]
    piece = near_ref.shape[1]
    me_row = lax.axis_index("row")
    core, chip = me_row % 2, me_row // 2
    for shift in range(chips):
        owner = (chip + shift) % chips
        near_ref[shift] = acc_ref[pl.ds(pl.multiple_of((owner * 2 + core) * piece, 8), piece), :]
        far_ref[shift] = acc_ref[pl.ds(pl.multiple_of((owner * 2 + 1 - core) * piece, 8), piece), :].astype(
            far_ref.dtype
        )


SMEM = pl.BlockSpec(memory_space=pltpu.SMEM)
VMEM = pl.BlockSpec(memory_space=pltpu.VMEM)


def tile_products(rows, cols, info, blocks, near, far, parts):
    out_rows = parts[0] * parts[1]
    chunk = parts[1]
    width = near.shape[2]
    return pl.pallas_call(
        forward_kernel,
        out_shape=(
            jax.ShapeDtypeStruct((chunk, width), jnp.float32),
            jax.ShapeDtypeStruct((parts[0], chunk, width), jnp.bfloat16),
        ),
        in_specs=[SMEM, SMEM, SMEM, VMEM, VMEM, VMEM],
        out_specs=(VMEM, VMEM),
        scratch_shapes=[
            pltpu.VMEM((2 * near.shape[0] * near.shape[1], width), jnp.bfloat16),
            pltpu.VMEM((out_rows, width), jnp.float32),
        ],
    )(rows, cols, info, blocks, near, far)


def tile_products_t(rows, cols, info, blocks, mine, got, n_out, out_rows):
    chunk = out_rows // n_out
    width = mine.shape[1]
    near = jax.ShapeDtypeStruct((n_out // 2, chunk, width), jnp.float32)
    far = jax.ShapeDtypeStruct((n_out // 2, chunk, width), jnp.bfloat16)
    return pl.pallas_call(
        functools.partial(backward_kernel, len(got) + 1),
        out_shape=(near, far),
        in_specs=[SMEM, SMEM, SMEM, VMEM, VMEM] + [VMEM] * len(got),
        out_specs=(VMEM, VMEM),
        scratch_shapes=[
            pltpu.VMEM(((len(got) + 1) * mine.shape[0], width), jnp.bfloat16),
            pltpu.VMEM((out_rows, width), jnp.float32),
        ],
    )(rows, cols, info, blocks, mine, *got)


def shifts(axis):
    n = lax.axis_size(axis)
    return [[(i, (i + shift) % n) for i in range(n)] for shift in range(1, n)]


def chip_shifts(n):
    chips = n // 2
    return [[(i, ((i // 2 + shift) % chips) * 2 + i % 2) for i in range(n)] for shift in range(1, chips)]


def partner(n):
    return [(i, i ^ 1) for i in range(n)]


def on_device(features, edge_tiles, tile_rows, tile_cols, tile_count, weight, cotangent):
    blocks = edge_tiles[0, 0]
    row_slots = tile_rows[0, 0]
    col_slots = tile_cols[0, 0]
    n_row = lax.axis_size("row")
    n_col = lax.axis_size("col")
    own_rows = features.shape[0]

    near = jnp.stack([features] + [lax.ppermute(features, "row", perm) for perm in chip_shifts(n_row)])
    far = lax.ppermute(near, "row", partner(n_row))
    info = tile_count.reshape(1)
    own, *send = tile_products(row_slots, col_slots, info, blocks, near, far, (n_col, own_rows))
    got = lax.all_to_all(send[0], "col", 0, 0, tiled=False)
    total = own + got.astype(jnp.float32).sum(0)
    activated, pulled_own = dense_layer(total, cotangent, weight)
    got = [lax.ppermute(pulled_own, "col", perm) for perm in shifts("col")]
    near_g, far_g = tile_products_t(
        row_slots, col_slots, info, blocks, pulled_own, got, n_row, n_row * own_rows
    )
    chip_sums = near_g + lax.ppermute(far_g, "row", partner(n_row)).astype(jnp.float32)
    total_g = chip_sums[0]
    for shift, perm in enumerate(chip_shifts(n_row)):
        piece = chip_sums[shift + 1].astype(jnp.bfloat16)
        total_g = total_g + lax.ppermute(piece, "row", perm).astype(jnp.float32)
    return (activated, total_g.astype(jnp.bfloat16))


def solution(mesh):
    return jax.shard_map(
        on_device,
        mesh=mesh,
        in_specs=(
            P(("col", "row"), None),
            P("row", "col", None, None, None),
            P("row", "col", None),
            P("row", "col", None),
            P("row", "col"),
            P(),
            P(("row", "col"), None),
        ),
        out_specs=(P(("row", "col"), None), P(("col", "row"), None)),
        check_vma=False,
    )
```

```python
import functools

import jax
import jax.numpy as jnp
from jax import lax
from jax.experimental import pallas as pl
from jax.experimental.pallas import tpu as pltpu
from jax.sharding import PartitionSpec as P


def silu_slope(mixed):
    sigma = jax.nn.sigmoid(mixed)
    return sigma * (1.0 + mixed * (1.0 - sigma))


def dense_layer(summed, grad_rows, weight):
    aggregated = summed.astype(jnp.bfloat16)
    mixed = jnp.dot(aggregated, weight, preferred_element_type=jnp.float32)
    activated = jax.nn.silu(mixed).astype(jnp.bfloat16)
    scaled = (grad_rows.astype(jnp.float32) * silu_slope(mixed)).astype(jnp.bfloat16)
    pulled = jnp.dot(scaled, weight.T, preferred_element_type=jnp.float32).astype(jnp.bfloat16)
    return (activated, pulled)


UNROLL = 4


def gather_peer(i, step, n):
    return i ^ step if n & (n - 1) == 0 else (i + step) % n


def gather_source(i, step, n):
    return i ^ step if n & (n - 1) == 0 else (i - step + n) % n


def run_slots(count, product, place):
    def group(g, carry):
        base = g * UNROLL
        values = [product(base + j) for j in range(UNROLL)]
        for j, value in enumerate(values):
            place(base + j, value)
        return carry

    def single(k, carry):
        place(k, product(k))
        return carry

    lax.fori_loop(0, count // UNROLL, group, 0)
    lax.fori_loop((count // UNROLL) * UNROLL, count, single, 0)


def split_out(acc_ref, own_ref, send_refs, me):
    chunk = own_ref.shape[0]
    n = len(send_refs) + 1
    own_ref[...] = acc_ref[pl.ds(pl.multiple_of(me * chunk, 8), chunk), :]
    for shift in range(1, n):
        start = pl.multiple_of(((me + shift) % n) * chunk, 8)
        send_refs[shift - 1][...] = acc_ref[pl.ds(start, chunk), :].astype(send_refs[shift - 1].dtype)


def forward_kernel(rows_ref, cols_ref, info_ref, a_ref, near_ref, far_ref, own_ref, *rest):
    send_refs, f_ref, acc_ref = rest[:-2], rest[-2], rest[-1]
    tile = a_ref.shape[1]
    chips, piece = near_ref.shape[0], near_ref.shape[1]
    me = lax.axis_index("row")
    core, chip = me % 2, me // 2
    for shift in range(chips):
        owner = (chip - shift + chips) % chips
        near = pl.multiple_of((owner * 2 + core) * piece, 16)
        far = pl.multiple_of((owner * 2 + 1 - core) * piece, 16)
        f_ref[pl.ds(near, piece), :] = near_ref[shift]
        f_ref[pl.ds(far, piece), :] = far_ref[shift]
    acc_ref[...] = jnp.zeros_like(acc_ref)

    def product(k):
        f = f_ref[pl.ds(pl.multiple_of(cols_ref[k] * tile, tile), tile), :]
        return jnp.dot(a_ref[k], f, preferred_element_type=jnp.float32)

    def place(k, value):
        rows = pl.ds(pl.multiple_of(rows_ref[k] * tile, tile), tile)
        acc_ref[rows, :] += value

    run_slots(jnp.minimum(info_ref[0], a_ref.shape[0]), product, place)
    split_out(acc_ref, own_ref, send_refs, lax.axis_index("col"))


def backward_kernel(n, rows_ref, cols_ref, info_ref, a_ref, mine_ref, *rest):
    got_refs = rest[: n - 1]
    near_ref, far_ref, block_ref, acc_ref = rest[n - 1:]
    tile = a_ref.shape[1]
    chunk = mine_ref.shape[0]
    me = lax.axis_index("col")
    block_ref[pl.ds(pl.multiple_of(me * chunk, 16), chunk), :] = mine_ref[...]
    for shift in range(1, n):
        start = pl.multiple_of(gather_source(me, shift, n) * chunk, 16)
        block_ref[pl.ds(start, chunk), :] = got_refs[shift - 1][...]
    acc_ref[...] = jnp.zeros_like(acc_ref)

    def product(k):
        p = block_ref[pl.ds(pl.multiple_of(rows_ref[k] * tile, tile), tile), :]
        return lax.dot_general(
            a_ref[k], p, (((0,), (0,)), ((), ())), preferred_element_type=jnp.float32
        )

    def place(k, value):
        cols = pl.ds(pl.multiple_of(cols_ref[k] * tile, tile), tile)
        acc_ref[cols, :] += value

    run_slots(jnp.minimum(info_ref[0], a_ref.shape[0]), product, place)
    chips = near_ref.shape[0]
    piece = near_ref.shape[1]
    me_row = lax.axis_index("row")
    core, chip = me_row % 2, me_row // 2
    for shift in range(chips):
        owner = (chip + shift) % chips
        near_ref[shift] = acc_ref[pl.ds(pl.multiple_of((owner * 2 + core) * piece, 8), piece), :]
        far_ref[shift] = acc_ref[pl.ds(pl.multiple_of((owner * 2 + 1 - core) * piece, 8), piece), :].astype(
            far_ref.dtype
        )


SMEM = pl.BlockSpec(memory_space=pltpu.SMEM)
VMEM = pl.BlockSpec(memory_space=pltpu.VMEM)


def tile_products(rows, cols, info, blocks, near, far, parts):
    out_rows = parts[0] * parts[1]
    chunk = parts[1]
    width = near.shape[2]
    return pl.pallas_call(
        forward_kernel,
        out_shape=(jax.ShapeDtypeStruct((chunk, width), jnp.float32),)
        + (jax.ShapeDtypeStruct((chunk, width), jnp.bfloat16),) * (parts[0] - 1),
        in_specs=[SMEM, SMEM, SMEM, VMEM, VMEM, VMEM],
        out_specs=(VMEM,) * parts[0],
        scratch_shapes=[
            pltpu.VMEM((2 * near.shape[0] * near.shape[1], width), jnp.bfloat16),
            pltpu.VMEM((out_rows, width), jnp.float32),
        ],
    )(rows, cols, info, blocks, near, far)


def tile_products_t(rows, cols, info, blocks, mine, got, n_out, out_rows):
    chunk = out_rows // n_out
    width = mine.shape[1]
    near = jax.ShapeDtypeStruct((n_out // 2, chunk, width), jnp.float32)
    far = jax.ShapeDtypeStruct((n_out // 2, chunk, width), jnp.bfloat16)
    return pl.pallas_call(
        functools.partial(backward_kernel, len(got) + 1),
        out_shape=(near, far),
        in_specs=[SMEM, SMEM, SMEM, VMEM, VMEM] + [VMEM] * len(got),
        out_specs=(VMEM, VMEM),
        scratch_shapes=[
            pltpu.VMEM(((len(got) + 1) * mine.shape[0], width), jnp.bfloat16),
            pltpu.VMEM((out_rows, width), jnp.float32),
        ],
    )(rows, cols, info, blocks, mine, *got)


def shifts(axis):
    n = lax.axis_size(axis)
    return [[(i, (i + shift) % n) for i in range(n)] for shift in range(1, n)]


def chip_shifts(n):
    chips = n // 2
    return [[(i, ((i // 2 + shift) % chips) * 2 + i % 2) for i in range(n)] for shift in range(1, chips)]


def partner(n):
    return [(i, i ^ 1) for i in range(n)]


def on_device(features, edge_tiles, tile_rows, tile_cols, tile_count, weight, cotangent):
    blocks = edge_tiles[0, 0]
    row_slots = tile_rows[0, 0]
    col_slots = tile_cols[0, 0]
    n_row = lax.axis_size("row")
    n_col = lax.axis_size("col")
    own_rows = features.shape[0]

    near = jnp.stack([features] + [lax.ppermute(features, "row", perm) for perm in chip_shifts(n_row)])
    far = lax.ppermute(near, "row", partner(n_row))
    info = tile_count.reshape(1)
    own, *send = tile_products(row_slots, col_slots, info, blocks, near, far, (n_col, own_rows))
    total = own
    for shift, perm in enumerate(shifts("col")):
        total = total + lax.ppermute(send[shift], "col", perm).astype(jnp.float32)
    activated, pulled_own = dense_layer(total, cotangent, weight)
    got = [
        lax.ppermute(pulled_own, "col", [(i, gather_peer(i, shift, n_col)) for i in range(n_col)])
        for shift in range(1, n_col)
    ]
    near_g, far_g = tile_products_t(
        row_slots, col_slots, info, blocks, pulled_own, got, n_row, n_row * own_rows
    )
    chip_sums = near_g + lax.ppermute(far_g, "row", partner(n_row)).astype(jnp.float32)
    total_g = chip_sums[0]
    for shift, perm in enumerate(chip_shifts(n_row)):
        piece = chip_sums[shift + 1].astype(jnp.bfloat16)
        total_g = total_g + lax.ppermute(piece, "row", perm).astype(jnp.float32)
    return (activated, total_g.astype(jnp.bfloat16))


def solution(mesh):
    return jax.shard_map(
        on_device,
        mesh=mesh,
        in_specs=(
            P(("col", "row"), None),
            P("row", "col", None, None, None),
            P("row", "col", None),
            P("row", "col", None),
            P("row", "col"),
            P(),
            P(("row", "col"), None),
        ),
        out_specs=(P(("row", "col"), None), P(("col", "row"), None)),
        check_vma=False,
    )
```

```python
import functools

import jax
import jax.numpy as jnp
from jax import lax
from jax.experimental import pallas as pl
from jax.experimental.pallas import tpu as pltpu
from jax.sharding import PartitionSpec as P


def dense_kernel(n, own_ref, *rest):
    got_refs = rest[: n - 1]
    grad_ref, weight_ref, act_ref = rest[n - 1 : n + 2]
    pulled_refs = rest[n + 2 :]
    total = own_ref[...]
    for got in got_refs:
        total = total + got[...].astype(jnp.float32)
    weight = weight_ref[...]
    mixed = jnp.dot(total.astype(jnp.bfloat16), weight, preferred_element_type=jnp.float32)
    sigma = jax.nn.sigmoid(mixed)
    act_ref[...] = (mixed * sigma).astype(act_ref.dtype)
    slope = sigma * (1.0 + mixed * (1.0 - sigma))
    scaled = (grad_ref[...].astype(jnp.float32) * slope).astype(jnp.bfloat16)
    pulled = lax.dot_general(
        scaled, weight, (((1,), (1,)), ((), ())), preferred_element_type=jnp.float32
    ).astype(jnp.bfloat16)
    for pulled_ref in pulled_refs:
        pulled_ref[...] = pulled


def dense_layer_kernel(own, got, grad_rows, weight):
    shape = jax.ShapeDtypeStruct(own.shape, jnp.bfloat16)
    return pl.pallas_call(
        functools.partial(dense_kernel, len(got) + 1),
        out_shape=(shape,) * (len(got) + 2),
        in_specs=[VMEM] * (len(got) + 3),
        out_specs=(VMEM,) * (len(got) + 2),
    )(own, *got, grad_rows, weight)


UNROLL = 4


def run_slots(count, product, place):
    def group(g, carry):
        base = g * UNROLL
        values = [product(base + j) for j in range(UNROLL)]
        for j, value in enumerate(values):
            place(base + j, value)
        return carry

    def single(k, carry):
        place(k, product(k))
        return carry

    lax.fori_loop(0, count // UNROLL, group, 0)
    lax.fori_loop((count // UNROLL) * UNROLL, count, single, 0)


def split_out(acc_ref, own_ref, send_refs, me):
    chunk = own_ref.shape[0]
    n = len(send_refs) + 1
    own_ref[...] = acc_ref[pl.ds(pl.multiple_of(me * chunk, 8), chunk), :]
    for shift in range(1, n):
        start = pl.multiple_of(((me + shift) % n) * chunk, 8)
        send_refs[shift - 1][...] = acc_ref[pl.ds(start, chunk), :].astype(send_refs[shift - 1].dtype)


def forward_kernel(rows_ref, cols_ref, info_ref, a_ref, near_ref, far_ref, own_ref, *rest):
    send_refs, f_ref, acc_ref = rest[:-2], rest[-2], rest[-1]
    tile = a_ref.shape[1]
    chips, piece = near_ref.shape[0], near_ref.shape[1]
    me = lax.axis_index("row")
    core, chip = me % 2, me // 2
    for shift in range(chips):
        owner = (chip - shift + chips) % chips
        near = pl.multiple_of((owner * 2 + core) * piece, 16)
        far = pl.multiple_of((owner * 2 + 1 - core) * piece, 16)
        f_ref[pl.ds(near, piece), :] = near_ref[shift]
        f_ref[pl.ds(far, piece), :] = far_ref[shift]
    acc_ref[...] = jnp.zeros_like(acc_ref)

    def product(k):
        f = f_ref[pl.ds(pl.multiple_of(cols_ref[k] * tile, tile), tile), :]
        return jnp.dot(a_ref[k], f, preferred_element_type=jnp.float32)

    def place(k, value):
        rows = pl.ds(pl.multiple_of(rows_ref[k] * tile, tile), tile)
        acc_ref[rows, :] += value

    run_slots(jnp.minimum(info_ref[0], a_ref.shape[0]), product, place)
    split_out(acc_ref, own_ref, send_refs, lax.axis_index("col"))


def backward_kernel(n, rows_ref, cols_ref, info_ref, a_ref, mine_ref, *rest):
    got_refs = rest[: n - 1]
    near_ref, far_ref, block_ref, acc_ref = rest[n - 1:]
    tile = a_ref.shape[1]
    chunk = mine_ref.shape[0]
    me = lax.axis_index("col")
    block_ref[pl.ds(pl.multiple_of(me * chunk, 16), chunk), :] = mine_ref[...]
    for shift in range(1, n):
        start = pl.multiple_of(((me - shift + n) % n) * chunk, 16)
        block_ref[pl.ds(start, chunk), :] = got_refs[shift - 1][...]
    acc_ref[...] = jnp.zeros_like(acc_ref)

    def product(k):
        p = block_ref[pl.ds(pl.multiple_of(rows_ref[k] * tile, tile), tile), :]
        return lax.dot_general(
            a_ref[k], p, (((0,), (0,)), ((), ())), preferred_element_type=jnp.float32
        )

    def place(k, value):
        cols = pl.ds(pl.multiple_of(cols_ref[k] * tile, tile), tile)
        acc_ref[cols, :] += value

    run_slots(jnp.minimum(info_ref[0], a_ref.shape[0]), product, place)
    chips = near_ref.shape[0]
    piece = near_ref.shape[1]
    me_row = lax.axis_index("row")
    core, chip = me_row % 2, me_row // 2
    for shift in range(chips):
        owner = (chip + shift) % chips
        near_ref[shift] = acc_ref[pl.ds(pl.multiple_of((owner * 2 + core) * piece, 8), piece), :]
        far_ref[shift] = acc_ref[pl.ds(pl.multiple_of((owner * 2 + 1 - core) * piece, 8), piece), :].astype(
            far_ref.dtype
        )


SMEM = pl.BlockSpec(memory_space=pltpu.SMEM)
VMEM = pl.BlockSpec(memory_space=pltpu.VMEM)


def tile_products(rows, cols, info, blocks, near, far, parts):
    out_rows = parts[0] * parts[1]
    chunk = parts[1]
    width = near.shape[2]
    return pl.pallas_call(
        forward_kernel,
        out_shape=(jax.ShapeDtypeStruct((chunk, width), jnp.float32),)
        + (jax.ShapeDtypeStruct((chunk, width), jnp.bfloat16),) * (parts[0] - 1),
        in_specs=[SMEM, SMEM, SMEM, VMEM, VMEM, VMEM],
        out_specs=(VMEM,) * parts[0],
        scratch_shapes=[
            pltpu.VMEM((2 * near.shape[0] * near.shape[1], width), jnp.bfloat16),
            pltpu.VMEM((out_rows, width), jnp.float32),
        ],
    )(rows, cols, info, blocks, near, far)


def tile_products_t(rows, cols, info, blocks, mine, got, n_out, out_rows):
    chunk = out_rows // n_out
    width = mine.shape[1]
    near = jax.ShapeDtypeStruct((n_out // 2, chunk, width), jnp.float32)
    far = jax.ShapeDtypeStruct((n_out // 2, chunk, width), jnp.bfloat16)
    return pl.pallas_call(
        functools.partial(backward_kernel, len(got) + 1),
        out_shape=(near, far),
        in_specs=[SMEM, SMEM, SMEM, VMEM, VMEM] + [VMEM] * len(got),
        out_specs=(VMEM, VMEM),
        scratch_shapes=[
            pltpu.VMEM(((len(got) + 1) * mine.shape[0], width), jnp.bfloat16),
            pltpu.VMEM((out_rows, width), jnp.float32),
        ],
    )(rows, cols, info, blocks, mine, *got)


def shifts(axis):
    n = lax.axis_size(axis)
    return [[(i, (i + shift) % n) for i in range(n)] for shift in range(1, n)]


def chip_shifts(n):
    chips = n // 2
    return [[(i, ((i // 2 + shift) % chips) * 2 + i % 2) for i in range(n)] for shift in range(1, chips)]


def partner(n):
    return [(i, i ^ 1) for i in range(n)]


def on_device(features, edge_tiles, tile_rows, tile_cols, tile_count, weight, cotangent):
    blocks = edge_tiles[0, 0]
    row_slots = tile_rows[0, 0]
    col_slots = tile_cols[0, 0]
    n_row = lax.axis_size("row")
    n_col = lax.axis_size("col")
    own_rows = features.shape[0]

    near = jnp.stack([features] + [lax.ppermute(features, "row", perm) for perm in chip_shifts(n_row)])
    far = lax.ppermute(near, "row", partner(n_row))
    info = tile_count.reshape(1)
    own, *send = tile_products(row_slots, col_slots, info, blocks, near, far, (n_col, own_rows))
    got_f = [lax.ppermute(send[shift], "col", perm) for shift, perm in enumerate(shifts("col"))]
    activated, pulled_own, *pulled_out = dense_layer_kernel(own, got_f, cotangent, weight)
    got = [lax.ppermute(piece, "col", perm) for piece, perm in zip(pulled_out, shifts("col"))]
    near_g, far_g = tile_products_t(
        row_slots, col_slots, info, blocks, pulled_own, got, n_row, n_row * own_rows
    )
    chip_sums = near_g + lax.ppermute(far_g, "row", partner(n_row)).astype(jnp.float32)
    total_g = chip_sums[0]
    for shift, perm in enumerate(chip_shifts(n_row)):
        piece = chip_sums[shift + 1].astype(jnp.bfloat16)
        total_g = total_g + lax.ppermute(piece, "row", perm).astype(jnp.float32)
    return (activated, total_g.astype(jnp.bfloat16))


def solution(mesh):
    return jax.shard_map(
        on_device,
        mesh=mesh,
        in_specs=(
            P(("col", "row"), None),
            P("row", "col", None, None, None),
            P("row", "col", None),
            P("row", "col", None),
            P("row", "col"),
            P(),
            P(("row", "col"), None),
        ),
        out_specs=(P(("row", "col"), None), P(("col", "row"), None)),
        check_vma=False,
    )
```

```python
import functools

import jax
import jax.numpy as jnp
from jax import lax
from jax.experimental import pallas as pl
from jax.experimental.pallas import tpu as pltpu
from jax.sharding import PartitionSpec as P


def dense_kernel(n, own_ref, *rest):
    got_refs = rest[: n - 1]
    grad_ref, weight_ref, act_ref = rest[n - 1 : n + 2]
    pulled_refs = rest[n + 2 :]
    total = own_ref[...]
    for got in got_refs:
        total = total + got[...].astype(jnp.float32)
    weight = weight_ref[...]
    mixed = jnp.dot(total.astype(jnp.bfloat16), weight, preferred_element_type=jnp.float32)
    sigma = jax.nn.sigmoid(mixed)
    act_ref[...] = (mixed * sigma).astype(act_ref.dtype)
    slope = sigma * (1.0 + mixed * (1.0 - sigma))
    scaled = (grad_ref[...].astype(jnp.float32) * slope).astype(jnp.bfloat16)
    pulled = lax.dot_general(
        scaled, weight, (((1,), (1,)), ((), ())), preferred_element_type=jnp.float32
    ).astype(jnp.bfloat16)
    for pulled_ref in pulled_refs:
        pulled_ref[...] = pulled


def dense_layer_kernel(own, got, grad_rows, weight):
    shape = jax.ShapeDtypeStruct(own.shape, jnp.bfloat16)
    return pl.pallas_call(
        functools.partial(dense_kernel, len(got) + 1),
        out_shape=(shape,) * (len(got) + 2),
        in_specs=[VMEM] * (len(got) + 3),
        out_specs=(VMEM,) * (len(got) + 2),
    )(own, *got, grad_rows, weight)


UNROLL = 4


def run_slots(count, product, place):
    def group(g, carry):
        base = g * UNROLL
        values = [product(base + j) for j in range(UNROLL)]
        for j, value in enumerate(values):
            place(base + j, value)
        return carry

    def single(k, carry):
        place(k, product(k))
        return carry

    lax.fori_loop(0, count // UNROLL, group, 0)
    lax.fori_loop((count // UNROLL) * UNROLL, count, single, 0)


def split_out(acc_ref, own_ref, send_refs, me):
    chunk = own_ref.shape[0]
    n = len(send_refs) + 1
    own_ref[...] = acc_ref[pl.ds(pl.multiple_of(me * chunk, 8), chunk), :]
    for shift in range(1, n):
        start = pl.multiple_of(((me + shift) % n) * chunk, 8)
        send_refs[shift - 1][...] = acc_ref[pl.ds(start, chunk), :].astype(send_refs[shift - 1].dtype)


def forward_kernel(rows_ref, cols_ref, info_ref, a_ref, near_ref, far_ref, own_ref, *rest):
    send_refs, f_ref, acc_ref = rest[:-2], rest[-2], rest[-1]
    tile = a_ref.shape[1]
    chips, piece = near_ref.shape[0], near_ref.shape[1]
    me = lax.axis_index("row")
    core, chip = me % 2, me // 2
    for shift in range(chips):
        owner = (chip - shift + chips) % chips
        near = pl.multiple_of((owner * 2 + core) * piece, 16)
        far = pl.multiple_of((owner * 2 + 1 - core) * piece, 16)
        f_ref[pl.ds(near, piece), :] = near_ref[shift]
        f_ref[pl.ds(far, piece), :] = far_ref[shift]
    acc_ref[...] = jnp.zeros_like(acc_ref)

    def product(k):
        f = f_ref[pl.ds(pl.multiple_of(cols_ref[k] * tile, tile), tile), :]
        return jnp.dot(a_ref[k], f, preferred_element_type=jnp.float32)

    def place(k, value):
        rows = pl.ds(pl.multiple_of(rows_ref[k] * tile, tile), tile)
        acc_ref[rows, :] += value

    run_slots(jnp.minimum(info_ref[0], a_ref.shape[0]), product, place)
    split_out(acc_ref, own_ref, send_refs, lax.axis_index("col"))


def backward_kernel(n, rows_ref, cols_ref, info_ref, a_ref, mine_ref, *rest):
    got_refs = rest[: n - 1]
    near_ref, far_ref, block_ref, acc_ref = rest[n - 1:]
    tile = a_ref.shape[1]
    chunk = mine_ref.shape[0]
    me = lax.axis_index("col")
    block_ref[pl.ds(pl.multiple_of(me * chunk, 16), chunk), :] = mine_ref[...]
    for shift in range(1, n):
        start = pl.multiple_of(((me - shift + n) % n) * chunk, 16)
        block_ref[pl.ds(start, chunk), :] = got_refs[shift - 1][...]
    acc_ref[...] = jnp.zeros_like(acc_ref)

    def product(k):
        p = block_ref[pl.ds(pl.multiple_of(rows_ref[k] * tile, tile), tile), :]
        return lax.dot_general(
            a_ref[k], p, (((0,), (0,)), ((), ())), preferred_element_type=jnp.float32
        )

    def place(k, value):
        cols = pl.ds(pl.multiple_of(cols_ref[k] * tile, tile), tile)
        acc_ref[cols, :] += value

    run_slots(jnp.minimum(info_ref[0], a_ref.shape[0]), product, place)
    chips = near_ref.shape[0]
    piece = near_ref.shape[1]
    me_row = lax.axis_index("row")
    core, chip = me_row % 2, me_row // 2
    for shift in range(chips):
        owner = (chip + shift) % chips
        near_ref[shift] = acc_ref[pl.ds(pl.multiple_of((owner * 2 + core) * piece, 8), piece), :]
        far_ref[shift] = acc_ref[pl.ds(pl.multiple_of((owner * 2 + 1 - core) * piece, 8), piece), :].astype(
            far_ref.dtype
        )


SMEM = pl.BlockSpec(memory_space=pltpu.SMEM)
VMEM = pl.BlockSpec(memory_space=pltpu.VMEM)


def tile_products(rows, cols, info, blocks, near, far, parts):
    out_rows = parts[0] * parts[1]
    chunk = parts[1]
    width = near.shape[2]
    return pl.pallas_call(
        forward_kernel,
        out_shape=(jax.ShapeDtypeStruct((chunk, width), jnp.float32),)
        + (jax.ShapeDtypeStruct((chunk, width), jnp.bfloat16),) * (parts[0] - 1),
        in_specs=[SMEM, SMEM, SMEM, VMEM, VMEM, VMEM],
        out_specs=(VMEM,) * parts[0],
        scratch_shapes=[
            pltpu.VMEM((2 * near.shape[0] * near.shape[1], width), jnp.bfloat16),
            pltpu.VMEM((out_rows, width), jnp.float32),
        ],
    )(rows, cols, info, blocks, near, far)


def tile_products_t(rows, cols, info, blocks, mine, got, n_out, out_rows):
    chunk = out_rows // n_out
    width = mine.shape[1]
    near = jax.ShapeDtypeStruct((n_out // 2, chunk, width), jnp.float32)
    far = jax.ShapeDtypeStruct((n_out // 2, chunk, width), jnp.bfloat16)
    return pl.pallas_call(
        functools.partial(backward_kernel, len(got) + 1),
        out_shape=(near, far),
        in_specs=[SMEM, SMEM, SMEM, VMEM, VMEM] + [VMEM] * len(got),
        out_specs=(VMEM, VMEM),
        scratch_shapes=[
            pltpu.VMEM(((len(got) + 1) * mine.shape[0], width), jnp.bfloat16),
            pltpu.VMEM((out_rows, width), jnp.float32),
        ],
    )(rows, cols, info, blocks, mine, *got)


def shifts(axis):
    n = lax.axis_size(axis)
    return [[(i, (i + shift) % n) for i in range(n)] for shift in range(1, n)]


def chip_shifts(n):
    chips = n // 2
    return [[(i, ((i // 2 + shift) % chips) * 2 + i % 2) for i in range(n)] for shift in range(1, chips)]


def partner(n):
    return [(i, i ^ 1) for i in range(n)]


def on_device(features, edge_tiles, tile_rows, tile_cols, tile_count, weight, cotangent):
    blocks = edge_tiles[0, 0]
    row_slots = tile_rows[0, 0]
    col_slots = tile_cols[0, 0]
    n_row = lax.axis_size("row")
    n_col = lax.axis_size("col")
    own_rows = features.shape[0]

    where = lax.axis_index("row").astype(jnp.float32)
    copies = [
        features * (1.0 + 0.0 * (where + shift)).astype(features.dtype)
        for shift in range(1, len(chip_shifts(n_row)) + 1)
    ]
    near = jnp.stack(
        [features] + [lax.ppermute(c, "row", perm) for c, perm in zip(copies, chip_shifts(n_row))]
    )
    far = lax.ppermute(near, "row", partner(n_row))
    info = tile_count.reshape(1)
    own, *send = tile_products(row_slots, col_slots, info, blocks, near, far, (n_col, own_rows))
    got_f = [lax.ppermute(send[shift], "col", perm) for shift, perm in enumerate(shifts("col"))]
    activated, pulled_own, *pulled_out = dense_layer_kernel(own, got_f, cotangent, weight)
    got = [lax.ppermute(piece, "col", perm) for piece, perm in zip(pulled_out, shifts("col"))]
    near_g, far_g = tile_products_t(
        row_slots, col_slots, info, blocks, pulled_own, got, n_row, n_row * own_rows
    )
    chip_sums = near_g + lax.ppermute(far_g, "row", partner(n_row)).astype(jnp.float32)
    total_g = chip_sums[0]
    for shift, perm in enumerate(chip_shifts(n_row)):
        piece = chip_sums[shift + 1].astype(jnp.bfloat16)
        total_g = total_g + lax.ppermute(piece, "row", perm).astype(jnp.float32)
    return (activated, total_g.astype(jnp.bfloat16))


def solution(mesh):
    return jax.shard_map(
        on_device,
        mesh=mesh,
        in_specs=(
            P(("col", "row"), None),
            P("row", "col", None, None, None),
            P("row", "col", None),
            P("row", "col", None),
            P("row", "col"),
            P(),
            P(("row", "col"), None),
        ),
        out_specs=(P(("row", "col"), None), P(("col", "row"), None)),
        check_vma=False,
    )
```

```python
import functools

import jax
import jax.numpy as jnp
from jax import lax
from jax.experimental import pallas as pl
from jax.experimental.pallas import tpu as pltpu
from jax.sharding import PartitionSpec as P


def dense_kernel(n, own_ref, *rest):
    got_refs = rest[: n - 1]
    grad_ref, weight_ref, act_ref = rest[n - 1 : n + 2]
    pulled_refs = rest[n + 2 :]
    total = own_ref[...]
    for got in got_refs:
        total = total + got[...].astype(jnp.float32)
    weight = weight_ref[...]
    mixed = jnp.dot(total.astype(jnp.bfloat16), weight, preferred_element_type=jnp.float32)
    sigma = jax.nn.sigmoid(mixed)
    act_ref[...] = (mixed * sigma).astype(act_ref.dtype)
    slope = sigma * (1.0 + mixed * (1.0 - sigma))
    scaled = (grad_ref[...].astype(jnp.float32) * slope).astype(jnp.bfloat16)
    pulled = lax.dot_general(
        scaled, weight, (((1,), (1,)), ((), ())), preferred_element_type=jnp.float32
    ).astype(jnp.bfloat16)
    for pulled_ref in pulled_refs:
        pulled_ref[...] = pulled


def dense_layer_kernel(own, got, grad_rows, weight):
    shape = jax.ShapeDtypeStruct(own.shape, jnp.bfloat16)
    return pl.pallas_call(
        functools.partial(dense_kernel, len(got) + 1),
        out_shape=(shape,) * (len(got) + 2),
        in_specs=[VMEM] * (len(got) + 3),
        out_specs=(VMEM,) * (len(got) + 2),
    )(own, *got, grad_rows, weight)


UNROLL = 4


def run_slots(count, product, place):
    def group(g, carry):
        base = g * UNROLL
        values = [product(base + j) for j in range(UNROLL)]
        for j, value in enumerate(values):
            place(base + j, value)
        return carry

    def single(k, carry):
        place(k, product(k))
        return carry

    lax.fori_loop(0, count // UNROLL, group, 0)
    lax.fori_loop((count // UNROLL) * UNROLL, count, single, 0)


def split_out(acc_ref, own_ref, send_refs, me):
    chunk = own_ref.shape[0]
    n = len(send_refs) + 1
    own_ref[...] = acc_ref[pl.ds(pl.multiple_of(me * chunk, 8), chunk), :]
    for shift in range(1, n):
        start = pl.multiple_of(((me + shift) % n) * chunk, 8)
        send_refs[shift - 1][...] = acc_ref[pl.ds(start, chunk), :].astype(send_refs[shift - 1].dtype)


def forward_kernel(rows_ref, cols_ref, info_ref, a_ref, near_ref, far_ref, own_ref, *rest):
    send_refs, f_ref, acc_ref = rest[:-2], rest[-2], rest[-1]
    tile = a_ref.shape[1]
    chips, piece = near_ref.shape[0], near_ref.shape[1]
    me = lax.axis_index("row")
    core, chip = me % 2, me // 2
    for shift in range(chips):
        owner = (chip - shift + chips) % chips
        near = pl.multiple_of((owner * 2 + core) * piece, 16)
        far = pl.multiple_of((owner * 2 + 1 - core) * piece, 16)
        f_ref[pl.ds(near, piece), :] = near_ref[shift]
        f_ref[pl.ds(far, piece), :] = far_ref[shift]
    acc_ref[...] = jnp.zeros_like(acc_ref)

    def product(k):
        f = f_ref[pl.ds(pl.multiple_of(cols_ref[k] * tile, tile), tile), :]
        return jnp.dot(a_ref[k], f, preferred_element_type=jnp.float32)

    def place(k, value):
        rows = pl.ds(pl.multiple_of(rows_ref[k] * tile, tile), tile)
        acc_ref[rows, :] += value

    run_slots(jnp.minimum(info_ref[0], a_ref.shape[0]), product, place)
    split_out(acc_ref, own_ref, send_refs, lax.axis_index("col"))


def backward_kernel(n, rows_ref, cols_ref, info_ref, a_ref, mine_ref, *rest):
    got_refs = rest[: n - 1]
    near_ref, far_ref, block_ref, acc_ref = rest[n - 1:]
    tile = a_ref.shape[1]
    chunk = mine_ref.shape[0]
    me = lax.axis_index("col")
    block_ref[pl.ds(pl.multiple_of(me * chunk, 16), chunk), :] = mine_ref[...]
    for shift in range(1, n):
        start = pl.multiple_of(((me - shift + n) % n) * chunk, 16)
        block_ref[pl.ds(start, chunk), :] = got_refs[shift - 1][...]
    acc_ref[...] = jnp.zeros_like(acc_ref)

    def product(k):
        p = block_ref[pl.ds(pl.multiple_of(rows_ref[k] * tile, tile), tile), :]
        return lax.dot_general(
            a_ref[k], p, (((0,), (0,)), ((), ())), preferred_element_type=jnp.float32
        )

    def place(k, value):
        cols = pl.ds(pl.multiple_of(cols_ref[k] * tile, tile), tile)
        acc_ref[cols, :] += value

    run_slots(jnp.minimum(info_ref[0], a_ref.shape[0]), product, place)
    chips = near_ref.shape[0]
    piece = near_ref.shape[1]
    me_row = lax.axis_index("row")
    core, chip = me_row % 2, me_row // 2
    for shift in range(chips):
        owner = (chip + shift) % chips
        near_ref[shift] = acc_ref[pl.ds(pl.multiple_of((owner * 2 + core) * piece, 8), piece), :]
        far_ref[shift] = acc_ref[pl.ds(pl.multiple_of((owner * 2 + 1 - core) * piece, 8), piece), :].astype(
            far_ref.dtype
        )


SMEM = pl.BlockSpec(memory_space=pltpu.SMEM)
VMEM = pl.BlockSpec(memory_space=pltpu.VMEM)


def tile_products(rows, cols, info, blocks, near, far, parts):
    out_rows = parts[0] * parts[1]
    chunk = parts[1]
    width = near.shape[2]
    return pl.pallas_call(
        forward_kernel,
        out_shape=(jax.ShapeDtypeStruct((chunk, width), jnp.float32),)
        + (jax.ShapeDtypeStruct((chunk, width), jnp.bfloat16),) * (parts[0] - 1),
        in_specs=[SMEM, SMEM, SMEM, VMEM, VMEM, VMEM],
        out_specs=(VMEM,) * parts[0],
        scratch_shapes=[
            pltpu.VMEM((2 * near.shape[0] * near.shape[1], width), jnp.bfloat16),
            pltpu.VMEM((out_rows, width), jnp.float32),
        ],
    )(rows, cols, info, blocks, near, far)


def tile_products_t(rows, cols, info, blocks, mine, got, n_out, out_rows):
    chunk = out_rows // n_out
    width = mine.shape[1]
    near = jax.ShapeDtypeStruct((n_out // 2, chunk, width), jnp.float32)
    far = jax.ShapeDtypeStruct((n_out // 2, chunk, width), jnp.bfloat16)
    return pl.pallas_call(
        functools.partial(backward_kernel, len(got) + 1),
        out_shape=(near, far),
        in_specs=[SMEM, SMEM, SMEM, VMEM, VMEM] + [VMEM] * len(got),
        out_specs=(VMEM, VMEM),
        scratch_shapes=[
            pltpu.VMEM(((len(got) + 1) * mine.shape[0], width), jnp.bfloat16),
            pltpu.VMEM((out_rows, width), jnp.float32),
        ],
    )(rows, cols, info, blocks, mine, *got)


def shifts(axis):
    n = lax.axis_size(axis)
    return [[(i, (i + shift) % n) for i in range(n)] for shift in range(1, n)]


def chip_shifts(n):
    chips = n // 2
    return [[(i, ((i // 2 + shift) % chips) * 2 + i % 2) for i in range(n)] for shift in range(1, chips)]


def partner(n):
    return [(i, i ^ 1) for i in range(n)]


def on_device(features, edge_tiles, tile_rows, tile_cols, tile_count, weight, cotangent):
    blocks = edge_tiles[0, 0]
    row_slots = tile_rows[0, 0]
    col_slots = tile_cols[0, 0]
    n_row = lax.axis_size("row")
    n_col = lax.axis_size("col")
    own_rows = features.shape[0]

    near = jnp.stack([features] + [lax.ppermute(features, "row", perm) for perm in chip_shifts(n_row)])
    far = lax.ppermute(near, "row", partner(n_row))
    info = tile_count.reshape(1)
    own, *send = tile_products(row_slots, col_slots, info, blocks, near, far, (n_col, own_rows))
    got_f = [lax.ppermute(send[shift], "col", perm) for shift, perm in enumerate(shifts("col"))]
    total = own
    for piece in got_f:
        total = total + piece.astype(jnp.float32)
    mixed = jnp.dot(total.astype(jnp.bfloat16), weight, preferred_element_type=jnp.float32)
    activated = jax.nn.silu(mixed).astype(jnp.bfloat16)
    sigma = jax.nn.sigmoid(mixed)
    scaled = (cotangent.astype(jnp.float32) * (sigma * (1.0 + mixed * (1.0 - sigma)))).astype(jnp.bfloat16)
    pulled_own = jnp.dot(scaled, weight.T, preferred_element_type=jnp.float32).astype(jnp.bfloat16)
    where = lax.axis_index("col").astype(jnp.float32)
    pulled_out = [
        pulled_own * (1.0 + 0.0 * (where + shift)).astype(jnp.bfloat16) for shift in range(1, n_col)
    ]
    got = [lax.ppermute(piece, "col", perm) for piece, perm in zip(pulled_out, shifts("col"))]
    near_g, far_g = tile_products_t(
        row_slots, col_slots, info, blocks, pulled_own, got, n_row, n_row * own_rows
    )
    chip_sums = near_g + lax.ppermute(far_g, "row", partner(n_row)).astype(jnp.float32)
    total_g = chip_sums[0]
    for shift, perm in enumerate(chip_shifts(n_row)):
        piece = chip_sums[shift + 1].astype(jnp.bfloat16)
        total_g = total_g + lax.ppermute(piece, "row", perm).astype(jnp.float32)
    return (activated, total_g.astype(jnp.bfloat16))


def solution(mesh):
    return jax.shard_map(
        on_device,
        mesh=mesh,
        in_specs=(
            P(("col", "row"), None),
            P("row", "col", None, None, None),
            P("row", "col", None),
            P("row", "col", None),
            P("row", "col"),
            P(),
            P(("row", "col"), None),
        ),
        out_specs=(P(("row", "col"), None), P(("col", "row"), None)),
        check_vma=False,
    )
```

```python
import functools

import jax
import jax.numpy as jnp
from jax import lax
from jax.experimental import pallas as pl
from jax.experimental.pallas import tpu as pltpu
from jax.sharding import PartitionSpec as P


def dense_kernel(n, own_ref, *rest):
    got_refs = rest[: n - 1]
    grad_ref, weight_ref, act_ref = rest[n - 1 : n + 2]
    pulled_refs = rest[n + 2 :]
    total = own_ref[...]
    for got in got_refs:
        total = total + got[...].astype(jnp.float32)
    weight = weight_ref[...]
    mixed = jnp.dot(total.astype(jnp.bfloat16), weight, preferred_element_type=jnp.float32)
    sigma = jax.nn.sigmoid(mixed)
    act_ref[...] = (mixed * sigma).astype(act_ref.dtype)
    slope = sigma * (1.0 + mixed * (1.0 - sigma))
    scaled = (grad_ref[...].astype(jnp.float32) * slope).astype(jnp.bfloat16)
    pulled = lax.dot_general(
        scaled, weight, (((1,), (1,)), ((), ())), preferred_element_type=jnp.float32
    ).astype(jnp.bfloat16)
    for pulled_ref in pulled_refs:
        pulled_ref[...] = pulled


def dense_layer_kernel(own, got, grad_rows, weight):
    shape = jax.ShapeDtypeStruct(own.shape, jnp.bfloat16)
    return pl.pallas_call(
        functools.partial(dense_kernel, len(got) + 1),
        out_shape=(shape,) * (len(got) + 2),
        in_specs=[VMEM] * (len(got) + 3),
        out_specs=(VMEM,) * (len(got) + 2),
    )(own, *got, grad_rows, weight)


def chip_sum_kernel(near_ref, far_ref, own_ref, *send_refs):
    own_ref[...] = near_ref[0] + far_ref[0].astype(jnp.float32)
    for shift, send_ref in enumerate(send_refs, start=1):
        send_ref[...] = (near_ref[shift] + far_ref[shift].astype(jnp.float32)).astype(send_ref.dtype)


def chip_sums(near, far):
    piece = jax.ShapeDtypeStruct(near.shape[1:], jnp.bfloat16)
    return pl.pallas_call(
        chip_sum_kernel,
        out_shape=(jax.ShapeDtypeStruct(near.shape[1:], jnp.float32),) + (piece,) * (near.shape[0] - 1),
        in_specs=[VMEM, VMEM],
        out_specs=(VMEM,) * near.shape[0],
    )(near, far)


UNROLL = 4


def run_slots(count, product, place):
    def group(g, carry):
        base = g * UNROLL
        values = [product(base + j) for j in range(UNROLL)]
        for j, value in enumerate(values):
            place(base + j, value)
        return carry

    def single(k, carry):
        place(k, product(k))
        return carry

    lax.fori_loop(0, count // UNROLL, group, 0)
    lax.fori_loop((count // UNROLL) * UNROLL, count, single, 0)


def split_out(acc_ref, own_ref, send_refs, me):
    chunk = own_ref.shape[0]
    n = len(send_refs) + 1
    own_ref[...] = acc_ref[pl.ds(pl.multiple_of(me * chunk, 8), chunk), :]
    for shift in range(1, n):
        start = pl.multiple_of(((me + shift) % n) * chunk, 8)
        send_refs[shift - 1][...] = acc_ref[pl.ds(start, chunk), :].astype(send_refs[shift - 1].dtype)


def forward_kernel(rows_ref, cols_ref, info_ref, a_ref, near_ref, far_ref, own_ref, *rest):
    send_refs, f_ref, acc_ref = rest[:-2], rest[-2], rest[-1]
    tile = a_ref.shape[1]
    chips, piece = near_ref.shape[0], near_ref.shape[1]
    me = lax.axis_index("row")
    core, chip = me % 2, me // 2
    for shift in range(chips):
        owner = (chip - shift + chips) % chips
        near = pl.multiple_of((owner * 2 + core) * piece, 16)
        far = pl.multiple_of((owner * 2 + 1 - core) * piece, 16)
        f_ref[pl.ds(near, piece), :] = near_ref[shift]
        f_ref[pl.ds(far, piece), :] = far_ref[shift]
    acc_ref[...] = jnp.zeros_like(acc_ref)

    def product(k):
        f = f_ref[pl.ds(pl.multiple_of(cols_ref[k] * tile, tile), tile), :]
        return jnp.dot(a_ref[k], f, preferred_element_type=jnp.float32)

    def place(k, value):
        rows = pl.ds(pl.multiple_of(rows_ref[k] * tile, tile), tile)
        acc_ref[rows, :] += value

    run_slots(jnp.minimum(info_ref[0], a_ref.shape[0]), product, place)
    split_out(acc_ref, own_ref, send_refs, lax.axis_index("col"))


def backward_kernel(n, rows_ref, cols_ref, info_ref, a_ref, mine_ref, *rest):
    got_refs = rest[: n - 1]
    near_ref, far_ref, block_ref, acc_ref = rest[n - 1:]
    tile = a_ref.shape[1]
    chunk = mine_ref.shape[0]
    me = lax.axis_index("col")
    block_ref[pl.ds(pl.multiple_of(me * chunk, 16), chunk), :] = mine_ref[...]
    for shift in range(1, n):
        start = pl.multiple_of(((me - shift + n) % n) * chunk, 16)
        block_ref[pl.ds(start, chunk), :] = got_refs[shift - 1][...]
    acc_ref[...] = jnp.zeros_like(acc_ref)

    def product(k):
        p = block_ref[pl.ds(pl.multiple_of(rows_ref[k] * tile, tile), tile), :]
        return lax.dot_general(
            a_ref[k], p, (((0,), (0,)), ((), ())), preferred_element_type=jnp.float32
        )

    def place(k, value):
        cols = pl.ds(pl.multiple_of(cols_ref[k] * tile, tile), tile)
        acc_ref[cols, :] += value

    run_slots(jnp.minimum(info_ref[0], a_ref.shape[0]), product, place)
    chips = near_ref.shape[0]
    piece = near_ref.shape[1]
    me_row = lax.axis_index("row")
    core, chip = me_row % 2, me_row // 2
    for shift in range(chips):
        owner = (chip + shift) % chips
        near_ref[shift] = acc_ref[pl.ds(pl.multiple_of((owner * 2 + core) * piece, 8), piece), :]
        far_ref[shift] = acc_ref[pl.ds(pl.multiple_of((owner * 2 + 1 - core) * piece, 8), piece), :].astype(
            far_ref.dtype
        )


SMEM = pl.BlockSpec(memory_space=pltpu.SMEM)
VMEM = pl.BlockSpec(memory_space=pltpu.VMEM)


def tile_products(rows, cols, info, blocks, near, far, parts):
    out_rows = parts[0] * parts[1]
    chunk = parts[1]
    width = near.shape[2]
    return pl.pallas_call(
        forward_kernel,
        out_shape=(jax.ShapeDtypeStruct((chunk, width), jnp.float32),)
        + (jax.ShapeDtypeStruct((chunk, width), jnp.bfloat16),) * (parts[0] - 1),
        in_specs=[SMEM, SMEM, SMEM, VMEM, VMEM, VMEM],
        out_specs=(VMEM,) * parts[0],
        scratch_shapes=[
            pltpu.VMEM((2 * near.shape[0] * near.shape[1], width), jnp.bfloat16),
            pltpu.VMEM((out_rows, width), jnp.float32),
        ],
    )(rows, cols, info, blocks, near, far)


def tile_products_t(rows, cols, info, blocks, mine, got, n_out, out_rows):
    chunk = out_rows // n_out
    width = mine.shape[1]
    near = jax.ShapeDtypeStruct((n_out // 2, chunk, width), jnp.float32)
    far = jax.ShapeDtypeStruct((n_out // 2, chunk, width), jnp.bfloat16)
    return pl.pallas_call(
        functools.partial(backward_kernel, len(got) + 1),
        out_shape=(near, far),
        in_specs=[SMEM, SMEM, SMEM, VMEM, VMEM] + [VMEM] * len(got),
        out_specs=(VMEM, VMEM),
        scratch_shapes=[
            pltpu.VMEM(((len(got) + 1) * mine.shape[0], width), jnp.bfloat16),
            pltpu.VMEM((out_rows, width), jnp.float32),
        ],
    )(rows, cols, info, blocks, mine, *got)


def shifts(axis):
    n = lax.axis_size(axis)
    return [[(i, (i + shift) % n) for i in range(n)] for shift in range(1, n)]


def chip_shifts(n):
    chips = n // 2
    return [[(i, ((i // 2 + shift) % chips) * 2 + i % 2) for i in range(n)] for shift in range(1, chips)]


def partner(n):
    return [(i, i ^ 1) for i in range(n)]


def on_device(features, edge_tiles, tile_rows, tile_cols, tile_count, weight, cotangent):
    blocks = edge_tiles[0, 0]
    row_slots = tile_rows[0, 0]
    col_slots = tile_cols[0, 0]
    n_row = lax.axis_size("row")
    n_col = lax.axis_size("col")
    own_rows = features.shape[0]

    near = jnp.stack([features] + [lax.ppermute(features, "row", perm) for perm in chip_shifts(n_row)])
    far = lax.ppermute(near, "row", partner(n_row))
    info = tile_count.reshape(1)
    own, *send = tile_products(row_slots, col_slots, info, blocks, near, far, (n_col, own_rows))
    got_f = [lax.ppermute(send[shift], "col", perm) for shift, perm in enumerate(shifts("col"))]
    activated, pulled_own, *pulled_out = dense_layer_kernel(own, got_f, cotangent, weight)
    got = [lax.ppermute(piece, "col", perm) for piece, perm in zip(pulled_out, shifts("col"))]
    near_g, far_g = tile_products_t(
        row_slots, col_slots, info, blocks, pulled_own, got, n_row, n_row * own_rows
    )
    total_g, *pieces = chip_sums(near_g, lax.ppermute(far_g, "row", partner(n_row)))
    for piece, perm in zip(pieces, chip_shifts(n_row)):
        total_g = total_g + lax.ppermute(piece, "row", perm).astype(jnp.float32)
    return (activated, total_g.astype(jnp.bfloat16))


def solution(mesh):
    return jax.shard_map(
        on_device,
        mesh=mesh,
        in_specs=(
            P(("col", "row"), None),
            P("row", "col", None, None, None),
            P("row", "col", None),
            P("row", "col", None),
            P("row", "col"),
            P(),
            P(("row", "col"), None),
        ),
        out_specs=(P(("row", "col"), None), P(("col", "row"), None)),
        check_vma=False,
    )
```

```python
import functools

import jax
import jax.numpy as jnp
from jax import lax
from jax.experimental import pallas as pl
from jax.experimental.pallas import tpu as pltpu
from jax.sharding import PartitionSpec as P


def dense_kernel(n, own_ref, *rest):
    got_refs = rest[: n - 1]
    grad_ref, weight_ref, act_ref = rest[n - 1 : n + 2]
    pulled_refs = rest[n + 2 :]
    total = own_ref[...]
    for got in got_refs:
        total = total + got[...].astype(jnp.float32)
    weight = weight_ref[...]
    mixed = jnp.dot(total.astype(jnp.bfloat16), weight, preferred_element_type=jnp.float32)
    sigma = jax.nn.sigmoid(mixed)
    act_ref[...] = (mixed * sigma).astype(act_ref.dtype)
    slope = sigma * (1.0 + mixed * (1.0 - sigma))
    scaled = (grad_ref[...].astype(jnp.float32) * slope).astype(jnp.bfloat16)
    pulled = lax.dot_general(
        scaled, weight, (((1,), (1,)), ((), ())), preferred_element_type=jnp.float32
    ).astype(jnp.bfloat16)
    for pulled_ref in pulled_refs:
        pulled_ref[...] = pulled


def dense_layer_kernel(own, got, grad_rows, weight):
    shape = jax.ShapeDtypeStruct(own.shape, jnp.bfloat16)
    return pl.pallas_call(
        functools.partial(dense_kernel, len(got) + 1),
        out_shape=(shape,) * (len(got) + 2),
        in_specs=[VMEM] * (len(got) + 3),
        out_specs=(VMEM,) * (len(got) + 2),
    )(own, *got, grad_rows, weight)


UNROLL = 6


def run_slots(count, product, place):
    def group(g, carry):
        base = g * UNROLL
        values = [product(base + j) for j in range(UNROLL)]
        for j, value in enumerate(values):
            place(base + j, value)
        return carry

    def single(k, carry):
        place(k, product(k))
        return carry

    lax.fori_loop(0, count // UNROLL, group, 0)
    lax.fori_loop((count // UNROLL) * UNROLL, count, single, 0)


def split_out(acc_ref, own_ref, send_refs, me):
    chunk = own_ref.shape[0]
    n = len(send_refs) + 1
    own_ref[...] = acc_ref[pl.ds(pl.multiple_of(me * chunk, 8), chunk), :]
    for shift in range(1, n):
        start = pl.multiple_of(((me + shift) % n) * chunk, 8)
        send_refs[shift - 1][...] = acc_ref[pl.ds(start, chunk), :].astype(send_refs[shift - 1].dtype)


def forward_kernel(rows_ref, cols_ref, info_ref, a_ref, near_ref, far_ref, own_ref, *rest):
    send_refs, f_ref, acc_ref = rest[:-2], rest[-2], rest[-1]
    tile = a_ref.shape[1]
    chips, piece = near_ref.shape[0], near_ref.shape[1]
    me = lax.axis_index("row")
    core, chip = me % 2, me // 2
    for shift in range(chips):
        owner = (chip - shift + chips) % chips
        near = pl.multiple_of((owner * 2 + core) * piece, 16)
        far = pl.multiple_of((owner * 2 + 1 - core) * piece, 16)
        f_ref[pl.ds(near, piece), :] = near_ref[shift]
        f_ref[pl.ds(far, piece), :] = far_ref[shift]
    acc_ref[...] = jnp.zeros_like(acc_ref)

    def product(k):
        f = f_ref[pl.ds(pl.multiple_of(cols_ref[k] * tile, tile), tile), :]
        return jnp.dot(a_ref[k], f, preferred_element_type=jnp.float32)

    def place(k, value):
        rows = pl.ds(pl.multiple_of(rows_ref[k] * tile, tile), tile)
        acc_ref[rows, :] += value

    run_slots(jnp.minimum(info_ref[0], a_ref.shape[0]), product, place)
    split_out(acc_ref, own_ref, send_refs, lax.axis_index("col"))


def backward_kernel(n, rows_ref, cols_ref, info_ref, a_ref, mine_ref, *rest):
    got_refs = rest[: n - 1]
    near_ref, far_ref, block_ref, acc_ref = rest[n - 1:]
    tile = a_ref.shape[1]
    chunk = mine_ref.shape[0]
    me = lax.axis_index("col")
    block_ref[pl.ds(pl.multiple_of(me * chunk, 16), chunk), :] = mine_ref[...]
    for shift in range(1, n):
        start = pl.multiple_of(((me - shift + n) % n) * chunk, 16)
        block_ref[pl.ds(start, chunk), :] = got_refs[shift - 1][...]
    acc_ref[...] = jnp.zeros_like(acc_ref)

    def product(k):
        p = block_ref[pl.ds(pl.multiple_of(rows_ref[k] * tile, tile), tile), :]
        return lax.dot_general(
            a_ref[k], p, (((0,), (0,)), ((), ())), preferred_element_type=jnp.float32
        )

    def place(k, value):
        cols = pl.ds(pl.multiple_of(cols_ref[k] * tile, tile), tile)
        acc_ref[cols, :] += value

    run_slots(jnp.minimum(info_ref[0], a_ref.shape[0]), product, place)
    chips = near_ref.shape[0]
    piece = near_ref.shape[1]
    me_row = lax.axis_index("row")
    core, chip = me_row % 2, me_row // 2
    for shift in range(chips):
        owner = (chip + shift) % chips
        near_ref[shift] = acc_ref[pl.ds(pl.multiple_of((owner * 2 + core) * piece, 8), piece), :]
        far_ref[shift] = acc_ref[pl.ds(pl.multiple_of((owner * 2 + 1 - core) * piece, 8), piece), :].astype(
            far_ref.dtype
        )


SMEM = pl.BlockSpec(memory_space=pltpu.SMEM)
VMEM = pl.BlockSpec(memory_space=pltpu.VMEM)


def tile_products(rows, cols, info, blocks, near, far, parts):
    out_rows = parts[0] * parts[1]
    chunk = parts[1]
    width = near.shape[2]
    return pl.pallas_call(
        forward_kernel,
        out_shape=(jax.ShapeDtypeStruct((chunk, width), jnp.float32),)
        + (jax.ShapeDtypeStruct((chunk, width), jnp.bfloat16),) * (parts[0] - 1),
        in_specs=[SMEM, SMEM, SMEM, VMEM, VMEM, VMEM],
        out_specs=(VMEM,) * parts[0],
        scratch_shapes=[
            pltpu.VMEM((2 * near.shape[0] * near.shape[1], width), jnp.bfloat16),
            pltpu.VMEM((out_rows, width), jnp.float32),
        ],
    )(rows, cols, info, blocks, near, far)


def tile_products_t(rows, cols, info, blocks, mine, got, n_out, out_rows):
    chunk = out_rows // n_out
    width = mine.shape[1]
    near = jax.ShapeDtypeStruct((n_out // 2, chunk, width), jnp.float32)
    far = jax.ShapeDtypeStruct((n_out // 2, chunk, width), jnp.bfloat16)
    return pl.pallas_call(
        functools.partial(backward_kernel, len(got) + 1),
        out_shape=(near, far),
        in_specs=[SMEM, SMEM, SMEM, VMEM, VMEM] + [VMEM] * len(got),
        out_specs=(VMEM, VMEM),
        scratch_shapes=[
            pltpu.VMEM(((len(got) + 1) * mine.shape[0], width), jnp.bfloat16),
            pltpu.VMEM((out_rows, width), jnp.float32),
        ],
    )(rows, cols, info, blocks, mine, *got)


def shifts(axis):
    n = lax.axis_size(axis)
    return [[(i, (i + shift) % n) for i in range(n)] for shift in range(1, n)]


def chip_shifts(n):
    chips = n // 2
    return [[(i, ((i // 2 + shift) % chips) * 2 + i % 2) for i in range(n)] for shift in range(1, chips)]


def partner(n):
    return [(i, i ^ 1) for i in range(n)]


def on_device(features, edge_tiles, tile_rows, tile_cols, tile_count, weight, cotangent):
    blocks = edge_tiles[0, 0]
    row_slots = tile_rows[0, 0]
    col_slots = tile_cols[0, 0]
    n_row = lax.axis_size("row")
    n_col = lax.axis_size("col")
    own_rows = features.shape[0]

    near = jnp.stack([features] + [lax.ppermute(features, "row", perm) for perm in chip_shifts(n_row)])
    far = lax.ppermute(near, "row", partner(n_row))
    info = tile_count.reshape(1)
    own, *send = tile_products(row_slots, col_slots, info, blocks, near, far, (n_col, own_rows))
    got_f = [lax.ppermute(send[shift], "col", perm) for shift, perm in enumerate(shifts("col"))]
    activated, pulled_own, *pulled_out = dense_layer_kernel(own, got_f, cotangent, weight)
    got = [lax.ppermute(piece, "col", perm) for piece, perm in zip(pulled_out, shifts("col"))]
    near_g, far_g = tile_products_t(
        row_slots, col_slots, info, blocks, pulled_own, got, n_row, n_row * own_rows
    )
    chip_sums = near_g + lax.ppermute(far_g, "row", partner(n_row)).astype(jnp.float32)
    total_g = chip_sums[0]
    for shift, perm in enumerate(chip_shifts(n_row)):
        piece = chip_sums[shift + 1].astype(jnp.bfloat16)
        total_g = total_g + lax.ppermute(piece, "row", perm).astype(jnp.float32)
    return (activated, total_g.astype(jnp.bfloat16))


def solution(mesh):
    return jax.shard_map(
        on_device,
        mesh=mesh,
        in_specs=(
            P(("col", "row"), None),
            P("row", "col", None, None, None),
            P("row", "col", None),
            P("row", "col", None),
            P("row", "col"),
            P(),
            P(("row", "col"), None),
        ),
        out_specs=(P(("row", "col"), None), P(("col", "row"), None)),
        check_vma=False,
    )
```

```python
import functools

import jax
import jax.numpy as jnp
from jax import lax
from jax.experimental import pallas as pl
from jax.experimental.pallas import tpu as pltpu
from jax.sharding import PartitionSpec as P


def dense_kernel(n, own_ref, *rest):
    got_refs = rest[: n - 1]
    grad_ref, weight_ref, act_ref = rest[n - 1 : n + 2]
    pulled_refs = rest[n + 2 :]
    total = own_ref[...]
    for got in got_refs:
        total = total + got[...].astype(jnp.float32)
    weight = weight_ref[...]
    mixed = jnp.dot(total.astype(jnp.bfloat16), weight, preferred_element_type=jnp.float32)
    sigma = jax.nn.sigmoid(mixed)
    act_ref[...] = (mixed * sigma).astype(act_ref.dtype)
    slope = sigma * (1.0 + mixed * (1.0 - sigma))
    scaled = (grad_ref[...].astype(jnp.float32) * slope).astype(jnp.bfloat16)
    pulled = lax.dot_general(
        scaled, weight, (((1,), (1,)), ((), ())), preferred_element_type=jnp.float32
    ).astype(jnp.bfloat16)
    for pulled_ref in pulled_refs:
        pulled_ref[...] = pulled


def dense_layer_kernel(own, got, grad_rows, weight):
    shape = jax.ShapeDtypeStruct(own.shape, jnp.bfloat16)
    return pl.pallas_call(
        functools.partial(dense_kernel, len(got) + 1),
        out_shape=(shape,) * (len(got) + 2),
        in_specs=[VMEM] * (len(got) + 3),
        out_specs=(VMEM,) * (len(got) + 2),
    )(own, *got, grad_rows, weight)


UNROLL = 4


def run_slots(count, product, place):
    def group(g, carry):
        base = g * UNROLL
        values = [product(base + j) for j in range(UNROLL)]
        for j, value in enumerate(values):
            place(base + j, value)
        return carry

    def single(k, carry):
        place(k, product(k))
        return carry

    lax.fori_loop(0, count // UNROLL, group, 0)
    lax.fori_loop((count // UNROLL) * UNROLL, count, single, 0)


def split_out(acc_ref, own_ref, send_refs, me):
    chunk = own_ref.shape[0]
    n = len(send_refs) + 1
    own_ref[...] = acc_ref[pl.ds(pl.multiple_of(me * chunk, 8), chunk), :]
    for shift in range(1, n):
        start = pl.multiple_of(((me + shift) % n) * chunk, 8)
        send_refs[shift - 1][...] = acc_ref[pl.ds(start, chunk), :].astype(send_refs[shift - 1].dtype)


def forward_kernel(rows_ref, cols_ref, info_ref, a_ref, near_ref, far_ref, own_ref, *rest):
    send_refs, f_ref, acc_ref = rest[:-2], rest[-2], rest[-1]
    tile = a_ref.shape[1]
    chips, piece = near_ref.shape[0], near_ref.shape[1]
    me = lax.axis_index("row")
    core, chip = me % 2, me // 2
    for shift in range(chips):
        owner = (chip - shift + chips) % chips
        near = pl.multiple_of((owner * 2 + core) * piece, 16)
        far = pl.multiple_of((owner * 2 + 1 - core) * piece, 16)
        f_ref[pl.ds(near, piece), :] = near_ref[shift]
        f_ref[pl.ds(far, piece), :] = far_ref[shift]
    acc_ref[...] = jnp.zeros_like(acc_ref)

    def product(k):
        f = f_ref[pl.ds(pl.multiple_of(cols_ref[k] * tile, tile), tile), :]
        return jnp.dot(a_ref[k], f, preferred_element_type=jnp.float32)

    def place(k, value):
        rows = pl.ds(pl.multiple_of(rows_ref[k] * tile, tile), tile)
        acc_ref[rows, :] += value

    run_slots(jnp.minimum(info_ref[0], a_ref.shape[0]), product, place)
    split_out(acc_ref, own_ref, send_refs, lax.axis_index("col"))


def backward_kernel(n, rows_ref, cols_ref, info_ref, a_ref, mine_ref, *rest):
    got_refs = rest[: n - 1]
    own_ref, near_ref, far_ref, block_ref, acc_ref = rest[n - 1:]
    tile = a_ref.shape[1]
    chunk = mine_ref.shape[0]
    me = lax.axis_index("col")
    block_ref[pl.ds(pl.multiple_of(me * chunk, 16), chunk), :] = mine_ref[...]
    for shift in range(1, n):
        start = pl.multiple_of(((me - shift + n) % n) * chunk, 16)
        block_ref[pl.ds(start, chunk), :] = got_refs[shift - 1][...]
    acc_ref[...] = jnp.zeros_like(acc_ref)

    def product(k):
        p = block_ref[pl.ds(pl.multiple_of(rows_ref[k] * tile, tile), tile), :]
        return lax.dot_general(
            a_ref[k], p, (((0,), (0,)), ((), ())), preferred_element_type=jnp.float32
        )

    def place(k, value):
        cols = pl.ds(pl.multiple_of(cols_ref[k] * tile, tile), tile)
        acc_ref[cols, :] += value

    run_slots(jnp.minimum(info_ref[0], a_ref.shape[0]), product, place)
    chips = far_ref.shape[0]
    piece = far_ref.shape[1]
    me_row = lax.axis_index("row")
    core, chip = me_row % 2, me_row // 2
    own_ref[...] = acc_ref[pl.ds(pl.multiple_of(me_row * piece, 8), piece), :]
    for shift in range(chips):
        owner = (chip + shift) % chips
        if shift:
            near_ref[shift - 1] = acc_ref[
                pl.ds(pl.multiple_of((owner * 2 + core) * piece, 8), piece), :
            ].astype(near_ref.dtype)
        far_ref[shift] = acc_ref[pl.ds(pl.multiple_of((owner * 2 + 1 - core) * piece, 8), piece), :].astype(
            far_ref.dtype
        )


SMEM = pl.BlockSpec(memory_space=pltpu.SMEM)
VMEM = pl.BlockSpec(memory_space=pltpu.VMEM)


def tile_products(rows, cols, info, blocks, near, far, parts):
    out_rows = parts[0] * parts[1]
    chunk = parts[1]
    width = near.shape[2]
    return pl.pallas_call(
        forward_kernel,
        out_shape=(jax.ShapeDtypeStruct((chunk, width), jnp.float32),)
        + (jax.ShapeDtypeStruct((chunk, width), jnp.bfloat16),) * (parts[0] - 1),
        in_specs=[SMEM, SMEM, SMEM, VMEM, VMEM, VMEM],
        out_specs=(VMEM,) * parts[0],
        scratch_shapes=[
            pltpu.VMEM((2 * near.shape[0] * near.shape[1], width), jnp.bfloat16),
            pltpu.VMEM((out_rows, width), jnp.float32),
        ],
    )(rows, cols, info, blocks, near, far)


def tile_products_t(rows, cols, info, blocks, mine, got, n_out, out_rows):
    chunk = out_rows // n_out
    width = mine.shape[1]
    own = jax.ShapeDtypeStruct((chunk, width), jnp.float32)
    near = jax.ShapeDtypeStruct((n_out // 2 - 1, chunk, width), jnp.bfloat16)
    far = jax.ShapeDtypeStruct((n_out // 2, chunk, width), jnp.bfloat16)
    return pl.pallas_call(
        functools.partial(backward_kernel, len(got) + 1),
        out_shape=(own, near, far),
        in_specs=[SMEM, SMEM, SMEM, VMEM, VMEM] + [VMEM] * len(got),
        out_specs=(VMEM, VMEM, VMEM),
        scratch_shapes=[
            pltpu.VMEM(((len(got) + 1) * mine.shape[0], width), jnp.bfloat16),
            pltpu.VMEM((out_rows, width), jnp.float32),
        ],
    )(rows, cols, info, blocks, mine, *got)


def shifts(axis):
    n = lax.axis_size(axis)
    return [[(i, (i + shift) % n) for i in range(n)] for shift in range(1, n)]


def chip_shifts(n):
    chips = n // 2
    return [[(i, ((i // 2 + shift) % chips) * 2 + i % 2) for i in range(n)] for shift in range(1, chips)]


def partner(n):
    return [(i, i ^ 1) for i in range(n)]


def on_device(features, edge_tiles, tile_rows, tile_cols, tile_count, weight, cotangent):
    blocks = edge_tiles[0, 0]
    row_slots = tile_rows[0, 0]
    col_slots = tile_cols[0, 0]
    n_row = lax.axis_size("row")
    n_col = lax.axis_size("col")
    own_rows = features.shape[0]

    near = jnp.stack([features] + [lax.ppermute(features, "row", perm) for perm in chip_shifts(n_row)])
    far = lax.ppermute(near, "row", partner(n_row))
    info = tile_count.reshape(1)
    own, *send = tile_products(row_slots, col_slots, info, blocks, near, far, (n_col, own_rows))
    got_f = [lax.ppermute(send[shift], "col", perm) for shift, perm in enumerate(shifts("col"))]
    activated, pulled_own, *pulled_out = dense_layer_kernel(own, got_f, cotangent, weight)
    got = [lax.ppermute(piece, "col", perm) for piece, perm in zip(pulled_out, shifts("col"))]
    own_g, near_g, far_g = tile_products_t(
        row_slots, col_slots, info, blocks, pulled_own, got, n_row, n_row * own_rows
    )
    swapped = lax.ppermute(far_g, "row", partner(n_row)).astype(jnp.float32)
    total_g = own_g + swapped[0]
    for shift, perm in enumerate(chip_shifts(n_row)):
        piece = (near_g[shift].astype(jnp.float32) + swapped[shift + 1]).astype(jnp.bfloat16)
        total_g = total_g + lax.ppermute(piece, "row", perm).astype(jnp.float32)
    return (activated, total_g.astype(jnp.bfloat16))


def solution(mesh):
    return jax.shard_map(
        on_device,
        mesh=mesh,
        in_specs=(
            P(("col", "row"), None),
            P("row", "col", None, None, None),
            P("row", "col", None),
            P("row", "col", None),
            P("row", "col"),
            P(),
            P(("row", "col"), None),
        ),
        out_specs=(P(("row", "col"), None), P(("col", "row"), None)),
        check_vma=False,
    )
```
